256 devices in a mesh: row: 8 (over z), col: 32 (over y, x, core).
Axes of the slice: x: 4, y: 4, z: 8, core: 2. Of those that a mesh axis runs over, the one named last changes fastest.
Arguments:
- features: bfloat16 [32768, 128], P(('row', 'col')), may hold values from -6 to 6
- first_weight: bfloat16 [128, 512], replicated, may hold values from -0.5 to 0.5
- second_weight: bfloat16 [512, 128], replicated, may hold values from -0.25 to 0.25
- tile_rows: int32 [8, 32, 80], P('row', 'col'), may hold values from 0 to 31
- tile_cols: int32 [8, 32, 80], P('row', 'col'), may hold values from 0 to 7
- tile_live: int32 [8, 32], P('row', 'col'), may hold values from 1 to 80, as said below
- column_mask: int32 [8, 32, 80, 128], P('row', 'col'), may hold values 0 or 1
- edge_weight: bfloat16 [8, 32, 80, 128, 128], P('row', 'col'), may hold values from 0.049804688 to 1
- cotangent: bfloat16 [32768, 128], P(('row', 'col')), may hold values from -6 to 6
Outputs:
- output: bfloat16 [32768, 128], P(('row', 'col'))
- first_grad: float32 [128, 512], replicated
- second_grad: float32 [512, 128], replicated
The draws below stay inside these ranges and needn't reach their ends.
Inputs may be any that keep to these rules, and one draw needn't show every extreme that they name: `tile_live`: slots at or past a device's count are unused; every device of the last column group of the grid uses all 80.
All inputs are finite; a program needn't handle non-finite values. No bound on the sum of `column_mask` on one device may be relied on, other than what follows from the above.
Results may differ from the reference program's by a relative error of at most 0.014.
Values may be sent and summed in bfloat16 or wider, within the bound.
No kernel may reach another device: no remote copies, remote signals or barrier semaphores. Data moves between devices by JAX's collectives and lax.ppermute only.
A program may use at most 128 MiB of HBM per device.

```python
import math
import jax
import jax.numpy as jnp
from jax import lax

SLOTS = 80
BLOCK = 128
F_IN = 128
HID = 512
F_OUT = 128
GRID_ROWS = 8
GRID_COLS = 32
DEV_BLOCKS = 1
ROW_BLOCKS = 32
COL_BLOCKS = 8
NODES = 32768


def draw_tile_rows(key, part):
    return jax.random.randint(key, (GRID_ROWS, GRID_COLS, SLOTS), 0, ROW_BLOCKS, dtype=jnp.int32)


def draw_tile_cols(key, part):
    shape = (GRID_ROWS, GRID_COLS, SLOTS)
    near_cols = jax.random.randint(jax.random.fold_in(key, 11), shape, 0, DEV_BLOCKS, dtype=jnp.int32)
    far_cols = jax.random.randint(jax.random.fold_in(key, 12), shape, 0, COL_BLOCKS, dtype=jnp.int32)
    choose_far = jax.random.randint(jax.random.fold_in(key, 13), shape, 0, 2, dtype=jnp.int32)
    own_panel = jnp.arange(GRID_ROWS, dtype=jnp.int32)[:, None, None] * DEV_BLOCKS + near_cols
    return jnp.where(choose_far == 0, own_panel, far_cols).astype(jnp.int32)


def draw_tile_live(key, part):
    grid_col = jnp.zeros((GRID_ROWS, GRID_COLS), jnp.int32) + jnp.arange(GRID_COLS, dtype=jnp.int32)[None, :]
    dropped = (GRID_COLS - 1 - grid_col) * (3 * SLOTS) // (4 * max(GRID_COLS - 1, 1))
    jitter_count = jax.random.randint(jax.random.fold_in(key, 21), (GRID_ROWS, GRID_COLS), 0, max(SLOTS // 8, 1) + 1, dtype=jnp.int32)
    jitter_count = jitter_count * (grid_col < GRID_COLS - 1).astype(jnp.int32)
    return jnp.maximum(SLOTS - dropped - jitter_count, 1).astype(jnp.int32)


def with_ends(drawn, key, smallest, high):
    longest = drawn.shape.index(max(drawn.shape))
    spots = []
    for shift in (0, 1):
        where = [jax.random.randint(jax.random.fold_in(key, axis), (), 0, length) for axis, length in enumerate(drawn.shape)]
        where[longest] = (where[longest] + shift) % drawn.shape[longest]
        spots.append(tuple(where))
    return drawn.at[spots[0]].set(smallest).at[spots[1]].set(high)


def block_scale(own_key, extent, cuts, least, high):
    def one(axis_at, blocks):
        heights = jax.random.uniform(jax.random.fold_in(jax.random.fold_in(own_key, 6), axis_at), (blocks,), jnp.float32, least / len(cuts), high / len(cuts))
        return jnp.repeat(jnp.exp(heights), extent[axis_at] // blocks).reshape((-1,) + (1,) * (len(extent) - axis_at - 1))

    gain = one(*cuts[0])
    for cut in cuts[1:]:
        gain = gain * one(*cut)
    return gain


def centred(rng, dims, scale, most, shards=(), kind=jnp.bfloat16):
    values = scale * jax.random.normal(rng, dims, jnp.float32)
    if shards:
        values = values * block_scale(rng, dims, shards, -0.22, 0.18)
    return jnp.clip(values, -most, most).astype(kind)


def setup_inputs(seed: int = 0) -> dict:
    seeds = jax.random.split(jax.random.key(seed), 10)
    return {
        "features": centred(seeds[0], (NODES, F_IN), 1.0, 6.0, ((0, 256),)),
        "first_weight": centred(seeds[1], (F_IN, HID), F_IN ** -0.5, 0.5),
        "second_weight": centred(seeds[2], (HID, F_OUT), HID ** -0.5, 0.25),
        "tile_rows": draw_tile_rows(jax.random.fold_in(seeds[9], 71), 0),
        "tile_cols": draw_tile_cols(jax.random.fold_in(seeds[9], 71), 0),
        "tile_live": draw_tile_live(jax.random.fold_in(seeds[9], 71), 0),
        "column_mask": with_ends((jax.random.randint(seeds[6], (GRID_ROWS, GRID_COLS, SLOTS, BLOCK), 0, 2) < 1).astype(jnp.int32), jax.random.fold_in(seeds[6], 1), 0, 1),
        "edge_weight": jnp.clip(jnp.exp(math.log(1.0) - 2.9996462 * jax.random.uniform(seeds[7], (GRID_ROWS, GRID_COLS, SLOTS, BLOCK, BLOCK), jnp.float32) ** block_scale(seeds[7], (GRID_ROWS, GRID_COLS, SLOTS, BLOCK, BLOCK), ((0, 8), (1, 32)), -0.2, 0.2)), 0.049804688, 1.0).astype(jnp.bfloat16),
        "cotangent": centred(seeds[8], (NODES, F_OUT), 1.0, 6.0, ((0, 256),)),
    }


gelu_coef = math.sqrt(2.0 / math.pi)

def gelu_tanh(value):
    return 0.5 * value * (1.0 + jnp.tanh(gelu_coef * (value + 0.044715 * value * value * value)))

def gelu_slope(value):
    tanh_value = jnp.tanh(gelu_coef * (value + 0.044715 * value * value * value))
    return 0.5 * (1.0 + tanh_value) + 0.5 * value * (1.0 - tanh_value * tanh_value) * gelu_coef * (1.0 + 3.0 * 0.044715 * value * value)

def global_blocks(tile_rows, tile_cols):
    grid_row = jnp.arange(GRID_ROWS, dtype=jnp.int32)[:, None, None]
    grid_col = jnp.arange(GRID_COLS, dtype=jnp.int32)[None, :, None]
    row_blocks = grid_row * ROW_BLOCKS + tile_rows
    col_blocks = tile_cols // DEV_BLOCKS * ROW_BLOCKS + grid_col * DEV_BLOCKS + tile_cols % DEV_BLOCKS
    return (row_blocks.reshape(-1, SLOTS).astype(jnp.int32), col_blocks.reshape(-1, SLOTS).astype(jnp.int32))

def device_tiles(weight, live_mask, live_count):
    used = (jnp.arange(SLOTS, dtype=jnp.int32) < live_count).astype(jnp.float32)
    return weight.astype(jnp.float32) * live_mask.astype(jnp.float32)[:, None, :] * used[:, None, None]

def stacked(edge_weight, column_mask, tile_live, row_blocks, col_blocks, tile_rows):
    grid_index = jnp.zeros((GRID_ROWS, GRID_COLS), jnp.int32) + jnp.arange(GRID_ROWS, dtype=jnp.int32)[:, None]
    return (edge_weight.reshape(-1, SLOTS, BLOCK, BLOCK), column_mask.reshape(-1, SLOTS, BLOCK), tile_live.reshape(-1), row_blocks, col_blocks, tile_rows.reshape(-1, SLOTS).astype(jnp.int32), grid_index.reshape(-1).astype(jnp.int32))

def degrees(items):

    def accumulate(carried, device_item):
        weight, live_mask, live_count, rows_here, cols_here, local_rows, grid_row = device_item
        tiles = device_tiles(weight, live_mask, live_count)
        return (carried.at[rows_here].add(lax.optimization_barrier(jnp.sum(tiles, axis=2))), None)
    start = jnp.zeros((NODES // BLOCK, BLOCK), jnp.float32)
    carried, _ = lax.scan(accumulate, start, items)
    return carried.reshape(NODES)

def spread(items, source, transpose):
    feature_width = source.shape[1]
    source_blocks = source.astype(jnp.float32).reshape(NODES // BLOCK, BLOCK, feature_width)

    def accumulate(carried, device_item):
        weight, live_mask, live_count, rows_here, cols_here, local_rows, grid_row = device_item
        tiles = device_tiles(weight, live_mask, live_count)
        if transpose:
            contrib = jnp.einsum('sij,sif->sjf', tiles, source_blocks[rows_here])
            return (carried.at[cols_here].add(contrib), None)
        contrib = jnp.einsum('sij,sjf->sif', tiles, source_blocks[cols_here])
        return (carried.at[rows_here].add(contrib), None)
    start = jnp.zeros((NODES // BLOCK, BLOCK, feature_width), jnp.float32)
    carried, _ = lax.scan(accumulate, start, items)
    return carried.reshape(NODES, feature_width)

def spread_rounded(items, source):
    feature_width = source.shape[1]
    source_blocks = source.astype(jnp.float32).reshape(NODES // BLOCK, BLOCK, feature_width)

    def accumulate(carried, device_item):
        weight, live_mask, live_count, rows_here, cols_here, local_rows, grid_row = device_item
        tiles = device_tiles(weight, live_mask, live_count)
        contrib = jnp.einsum('sij,sjf->sif', tiles, source_blocks[cols_here])
        local_sum = jnp.zeros((ROW_BLOCKS, BLOCK, feature_width), jnp.float32).at[local_rows].add(contrib)
        rounded = lax.optimization_barrier(local_sum.astype(jnp.bfloat16)).astype(jnp.float32)
        offset = (grid_row * ROW_BLOCKS).astype(jnp.int32)
        zero_index = jnp.zeros((), jnp.int32)
        current = lax.dynamic_slice(carried, (offset, zero_index, zero_index), (ROW_BLOCKS, BLOCK, feature_width))
        return (lax.dynamic_update_slice(carried, current + rounded, (offset, zero_index, zero_index)), None)
    start = jnp.zeros((NODES // BLOCK, BLOCK, feature_width), jnp.float32)
    carried, _ = lax.scan(accumulate, start, items)
    return carried.reshape(NODES, feature_width)

def reference(features, first_weight, second_weight, tile_rows, tile_cols, tile_live, column_mask, edge_weight, cotangent):
    row_blocks, col_blocks = global_blocks(tile_rows, tile_cols)
    items = stacked(edge_weight, column_mask, tile_live, row_blocks, col_blocks, tile_rows)
    degree = degrees(items)
    row_scale = (1.0 / jnp.sqrt(1.0 + degree))[:, None]
    first_mix = (features.astype(jnp.float32) + row_scale * spread(items, features, False)).astype(jnp.bfloat16)
    first_pre = jnp.dot(first_mix, first_weight, preferred_element_type=jnp.float32)
    hidden = gelu_tanh(first_pre).astype(jnp.bfloat16)
    second_mix = (hidden.astype(jnp.float32) + row_scale * spread_rounded(items, hidden)).astype(jnp.bfloat16)
    output = jnp.dot(second_mix, second_weight, preferred_element_type=jnp.float32).astype(jnp.bfloat16)
    mix_grad = jnp.dot(cotangent, second_weight.T, preferred_element_type=jnp.float32)
    scaled_grad = (row_scale * mix_grad).astype(jnp.bfloat16)
    hidden_grad = mix_grad + spread(items, scaled_grad, True)
    pre_grad = (hidden_grad * gelu_slope(first_pre)).astype(jnp.bfloat16)
    node_scale = 1.0 / math.sqrt(NODES)
    second_grad = jnp.dot(second_mix.T, cotangent, preferred_element_type=jnp.float32) * node_scale
    first_grad = jnp.dot(first_mix.T, pre_grad, preferred_element_type=jnp.float32) * node_scale
    return (output, first_grad, second_grad)
```

```python
import functools
import math

import jax
import jax.numpy as jnp
from jax import lax
from jax.experimental import pallas as pl
from jax.experimental.pallas import tpu as pltpu
from jax.sharding import PartitionSpec as P

BLOCK = 128


gelu_coef = math.sqrt(2.0 / math.pi)


def gelu_tanh(value):
    return 0.5 * value * (1.0 + jnp.tanh(gelu_coef * (value + 0.044715 * value * value * value)))


def gelu_slope(value):
    tanh_value = jnp.tanh(gelu_coef * (value + 0.044715 * value * value * value))
    return 0.5 * (1.0 + tanh_value) + 0.5 * value * (1.0 - tanh_value * tanh_value) * gelu_coef * (
        1.0 + 3.0 * 0.044715 * value * value
    )


def _masked_tile(tiles_ref, mask_ref, s):
    return (tiles_ref[s].astype(jnp.float32) * mask_ref[s]).astype(jnp.bfloat16)


def _forward_kernel(with_degree, live_ref, rows_ref, cols_ref, tiles_ref, mask_ref, src_ref, *rest):
    if with_degree:
        out_ref, deg_ref, acc_ref, dacc_ref = rest
    else:
        out_ref, acc_ref = rest
    slots = tiles_ref.shape[0]
    n_dst = acc_ref.shape[0]
    n_src = src_ref.shape[0]
    acc_ref[...] = jnp.zeros_like(acc_ref)
    if with_degree:
        dacc_ref[...] = jnp.zeros_like(dacc_ref)
    ones = jnp.ones((8, BLOCK), jnp.bfloat16)

    def body(s, carry):
        r = jnp.clip(rows_ref[s], 0, n_dst - 1)
        c = jnp.clip(cols_ref[s], 0, n_src - 1)
        tile = _masked_tile(tiles_ref, mask_ref, s)
        acc_ref[r] += jnp.dot(tile, src_ref[c], preferred_element_type=jnp.float32)
        if with_degree:
            dacc_ref[r] += lax.dot_general(
                ones, tile, (((1,), (1,)), ((), ())), preferred_element_type=jnp.float32
            )
        return carry

    lax.fori_loop(0, jnp.clip(live_ref[0], 0, slots), body, 0)
    out_ref[...] = acc_ref[...].astype(out_ref.dtype)
    if with_degree:
        deg_ref[...] = dacc_ref[...]


def _transpose_kernel(live_ref, rows_ref, cols_ref, tiles_ref, mask_ref, src_ref, out_ref, acc_ref):
    slots = tiles_ref.shape[0]
    n_dst = acc_ref.shape[0]
    n_src = src_ref.shape[0]
    acc_ref[...] = jnp.zeros_like(acc_ref)

    def body(s, carry):
        r = jnp.clip(rows_ref[s], 0, n_src - 1)
        c = jnp.clip(cols_ref[s], 0, n_dst - 1)
        tile = _masked_tile(tiles_ref, mask_ref, s)
        acc_ref[c] += jnp.dot(src_ref[r], tile, preferred_element_type=jnp.float32)
        return carry

    lax.fori_loop(0, jnp.clip(live_ref[0], 0, slots), body, 0)
    out_ref[...] = acc_ref[...].astype(out_ref.dtype)


_SMEM = pl.BlockSpec(memory_space=pltpu.SMEM)
_VMEM = pl.BlockSpec(memory_space=pltpu.VMEM)


def forward_aggregate(live, rows, cols, tiles, mask, src, n_dst, with_degree):
    width = src.shape[-1]
    slots = tiles.shape[0]
    out_shape = [jax.ShapeDtypeStruct((n_dst, BLOCK, width), jnp.bfloat16)]
    scratch = [pltpu.VMEM((n_dst, BLOCK, width), jnp.float32)]
    if with_degree:
        out_shape.append(jax.ShapeDtypeStruct((n_dst, 8, BLOCK), jnp.float32))
        scratch.append(pltpu.VMEM((n_dst, 8, BLOCK), jnp.float32))
    flops = 2 * slots * BLOCK * BLOCK * (width + (8 if with_degree else 0))
    bytes_accessed = tiles.size * 2 + src.size * 2 + n_dst * BLOCK * width * 2
    return pl.pallas_call(
        functools.partial(_forward_kernel, with_degree),
        out_shape=tuple(out_shape),
        in_specs=[_SMEM, _SMEM, _SMEM, _VMEM, _VMEM, _VMEM],
        out_specs=tuple([_VMEM] * len(out_shape)),
        scratch_shapes=scratch,
        cost_estimate=pl.CostEstimate(flops=flops, bytes_accessed=bytes_accessed, transcendentals=0),
    )(live, rows, cols, tiles, mask, src)


def transpose_aggregate(live, rows, cols, tiles, mask, src_t, n_dst):
    width = src_t.shape[1]
    slots = tiles.shape[0]
    flops = 2 * slots * BLOCK * BLOCK * width
    bytes_accessed = tiles.size * 2 + src_t.size * 2 + n_dst * BLOCK * width * 2
    return pl.pallas_call(
        _transpose_kernel,
        out_shape=jax.ShapeDtypeStruct((n_dst, width, BLOCK), jnp.bfloat16),
        in_specs=[_SMEM, _SMEM, _SMEM, _VMEM, _VMEM, _VMEM],
        out_specs=_VMEM,
        scratch_shapes=[pltpu.VMEM((n_dst, width, BLOCK), jnp.float32)],
        cost_estimate=pl.CostEstimate(flops=flops, bytes_accessed=bytes_accessed, transcendentals=0),
    )(live, rows, cols, tiles, mask, src_t)


def gather_blocks(block, axis):
    n = lax.axis_size(axis)
    return lax.all_to_all(jnp.broadcast_to(block[None], (n,) + block.shape), axis, 0, 0, tiled=False)


def scatter_blocks(blocks, axis):
    return lax.all_to_all(blocks, axis, 0, 0, tiled=False)


def split_hi_lo(value):
    hi = value.astype(jnp.bfloat16)
    lo = (value - hi.astype(jnp.float32)).astype(jnp.bfloat16)
    return hi, lo


def local(
    features,
    first_weight,
    second_weight,
    tile_rows,
    tile_cols,
    tile_live,
    column_mask,
    edge_weight,
    cotangent,
):
    f32 = jnp.float32
    bf16 = jnp.bfloat16
    n_rows_axis = lax.axis_size("row")
    n_cols_axis = lax.axis_size("col")
    node_count = features.shape[0]
    row_groups = n_cols_axis * node_count // BLOCK
    col_groups = n_rows_axis * node_count // BLOCK

    live = tile_live.reshape(1)
    rows = tile_rows[0, 0]
    cols = tile_cols[0, 0]
    tiles = edge_weight[0, 0]
    mask = column_mask[0, 0].astype(f32)[:, None, :]

    x_panel = gather_blocks(features, "row")
    partial_in, partial_deg = forward_aggregate(
        live, rows, cols, tiles, mask, x_panel, row_groups, with_degree=True
    )
    deg_hi, deg_lo = split_hi_lo(partial_deg[:, 0, :])
    pad = jnp.zeros((row_groups, 14, BLOCK), bf16)
    packed = jnp.concatenate([partial_in, deg_hi[:, None, :], deg_lo[:, None, :], pad], axis=1)
    arrived = scatter_blocks(packed, "col").astype(f32)
    summed = jnp.sum(arrived, axis=0)
    summed_in = summed[:BLOCK]
    degree = summed[BLOCK] + summed[BLOCK + 1]
    row_scale = (1.0 / jnp.sqrt(1.0 + degree))[:, None]

    first_mix = (features.astype(f32) + row_scale * summed_in).astype(bf16)
    first_pre = jnp.dot(first_mix, first_weight, preferred_element_type=f32)
    hidden = gelu_tanh(first_pre).astype(bf16)
    projected = jnp.dot(hidden, second_weight, preferred_element_type=f32)

    scaled_t = (row_scale * cotangent.astype(f32)).astype(bf16).T
    grad_panel_t = gather_blocks(scaled_t, "col")
    partial_back_t = transpose_aggregate(live, rows, cols, tiles, mask, grad_panel_t, col_groups)
    returned_t = jnp.sum(scatter_blocks(partial_back_t, "row").astype(f32), axis=0)

    y_panel = gather_blocks(projected.astype(bf16), "row")
    (partial_y,) = forward_aggregate(live, rows, cols, tiles, mask, y_panel, row_groups, with_degree=False)
    summed_y = jnp.sum(scatter_blocks(partial_y, "col").astype(f32), axis=0)
    output = (projected + row_scale * summed_y).astype(bf16)

    hp = lax.Precision.HIGHEST
    combined = cotangent.astype(f32) + returned_t.T
    hidden_grad = jnp.dot(combined, second_weight.astype(f32).T, precision=hp, preferred_element_type=f32)
    pre_grad = (hidden_grad * gelu_slope(first_pre)).astype(bf16)
    first_term = jnp.dot(first_mix.T, pre_grad, preferred_element_type=f32)
    second_term = jnp.dot(hidden.astype(f32).T, combined, precision=hp, preferred_element_type=f32)

    node_scale = 1.0 / math.sqrt(node_count * n_rows_axis * n_cols_axis)
    n_dev = n_rows_axis * n_cols_axis
    flat = jnp.concatenate([first_term.reshape(-1), second_term.reshape(-1)]) * node_scale
    pieces = scatter_blocks(flat.reshape(n_dev, -1), ("row", "col"))
    reduced = jnp.sum(pieces, axis=0)
    everything = gather_blocks(reduced, ("row", "col")).reshape(-1)
    split = first_term.size
    first_grad = everything[:split].reshape(first_term.shape)
    second_grad = everything[split:].reshape(second_term.shape)
    return (output, first_grad, second_grad)


def solution(mesh):
    return jax.shard_map(
        local,
        mesh=mesh,
        in_specs=(
            P(("row", "col"), None),
            P(),
            P(),
            P("row", "col", None),
            P("row", "col", None),
            P("row", "col"),
            P("row", "col", None, None),
            P("row", "col", None, None, None),
            P(("row", "col"), None),
        ),
        out_specs=(P(("row", "col"), None), P(), P()),
        check_vma=False,
    )
```

```python
import functools
import math

import jax
import jax.numpy as jnp
from jax import lax
from jax.experimental import pallas as pl
from jax.experimental.pallas import tpu as pltpu
from jax.sharding import PartitionSpec as P

BLOCK = 128


gelu_coef = math.sqrt(2.0 / math.pi)


def gelu_tanh(value):
    return 0.5 * value * (1.0 + jnp.tanh(gelu_coef * (value + 0.044715 * value * value * value)))


def gelu_slope(value):
    tanh_value = jnp.tanh(gelu_coef * (value + 0.044715 * value * value * value))
    return 0.5 * (1.0 + tanh_value) + 0.5 * value * (1.0 - tanh_value * tanh_value) * gelu_coef * (
        1.0 + 3.0 * 0.044715 * value * value
    )


def _masked_tile(tiles_ref, mask_ref, s):
    return (tiles_ref[s].astype(jnp.float32) * mask_ref[s]).astype(jnp.bfloat16)


def _forward_kernel(with_degree, live_ref, rows_ref, cols_ref, tiles_ref, mask_ref, src_ref, *rest):
    if with_degree:
        out_ref, deg_ref, acc_ref, dacc_ref = rest
    else:
        out_ref, acc_ref = rest
    slots = tiles_ref.shape[0]
    n_dst = acc_ref.shape[0]
    n_src = src_ref.shape[0]
    acc_ref[...] = jnp.zeros_like(acc_ref)
    if with_degree:
        dacc_ref[...] = jnp.zeros_like(dacc_ref)
    ones = jnp.ones((8, BLOCK), jnp.bfloat16)

    def body(s, carry):
        r = jnp.clip(rows_ref[s], 0, n_dst - 1)
        c = jnp.clip(cols_ref[s], 0, n_src - 1)
        tile = _masked_tile(tiles_ref, mask_ref, s)
        acc_ref[r] += jnp.dot(tile, src_ref[c], preferred_element_type=jnp.float32)
        if with_degree:
            dacc_ref[r] += lax.dot_general(
                ones, tile, (((1,), (1,)), ((), ())), preferred_element_type=jnp.float32
            )
        return carry

    lax.fori_loop(0, jnp.clip(live_ref[0], 0, slots), body, 0)
    out_ref[...] = acc_ref[...].astype(out_ref.dtype)
    if with_degree:
        deg_ref[...] = dacc_ref[...]


def _transpose_kernel(live_ref, rows_ref, cols_ref, tiles_ref, mask_ref, src_ref, out_ref, acc_ref):
    slots = tiles_ref.shape[0]
    n_dst = acc_ref.shape[0]
    n_src = src_ref.shape[0]
    acc_ref[...] = jnp.zeros_like(acc_ref)

    def body(s, carry):
        r = jnp.clip(rows_ref[s], 0, n_src - 1)
        c = jnp.clip(cols_ref[s], 0, n_dst - 1)
        tile = _masked_tile(tiles_ref, mask_ref, s)
        acc_ref[c] += jnp.dot(src_ref[r], tile, preferred_element_type=jnp.float32)
        return carry

    lax.fori_loop(0, jnp.clip(live_ref[0], 0, slots), body, 0)
    out_ref[...] = acc_ref[...].astype(out_ref.dtype)


_SMEM = pl.BlockSpec(memory_space=pltpu.SMEM)
_VMEM = pl.BlockSpec(memory_space=pltpu.VMEM)


def forward_aggregate(live, rows, cols, tiles, mask, src, n_dst, with_degree):
    width = src.shape[-1]
    slots = tiles.shape[0]
    out_shape = [jax.ShapeDtypeStruct((n_dst, BLOCK, width), jnp.bfloat16)]
    scratch = [pltpu.VMEM((n_dst, BLOCK, width), jnp.float32)]
    if with_degree:
        out_shape.append(jax.ShapeDtypeStruct((n_dst, 8, BLOCK), jnp.float32))
        scratch.append(pltpu.VMEM((n_dst, 8, BLOCK), jnp.float32))
    flops = 2 * slots * BLOCK * BLOCK * (width + (8 if with_degree else 0))
    bytes_accessed = tiles.size * 2 + src.size * 2 + n_dst * BLOCK * width * 2
    return pl.pallas_call(
        functools.partial(_forward_kernel, with_degree),
        out_shape=tuple(out_shape),
        in_specs=[_SMEM, _SMEM, _SMEM, _VMEM, _VMEM, _VMEM],
        out_specs=tuple([_VMEM] * len(out_shape)),
        scratch_shapes=scratch,
        cost_estimate=pl.CostEstimate(flops=flops, bytes_accessed=bytes_accessed, transcendentals=0),
    )(live, rows, cols, tiles, mask, src)


def transpose_aggregate(live, rows, cols, tiles, mask, src_t, n_dst):
    width = src_t.shape[1]
    slots = tiles.shape[0]
    flops = 2 * slots * BLOCK * BLOCK * width
    bytes_accessed = tiles.size * 2 + src_t.size * 2 + n_dst * BLOCK * width * 2
    return pl.pallas_call(
        _transpose_kernel,
        out_shape=jax.ShapeDtypeStruct((n_dst, width, BLOCK), jnp.bfloat16),
        in_specs=[_SMEM, _SMEM, _SMEM, _VMEM, _VMEM, _VMEM],
        out_specs=_VMEM,
        scratch_shapes=[pltpu.VMEM((n_dst, width, BLOCK), jnp.float32)],
        cost_estimate=pl.CostEstimate(flops=flops, bytes_accessed=bytes_accessed, transcendentals=0),
    )(live, rows, cols, tiles, mask, src_t)


def gather_blocks(block, axis):
    n = lax.axis_size(axis)
    return lax.all_to_all(jnp.broadcast_to(block[None], (n,) + block.shape), axis, 0, 0, tiled=False)


def scatter_blocks(blocks, axis):
    return lax.all_to_all(blocks, axis, 0, 0, tiled=False)


def split_hi_lo(value):
    hi = value.astype(jnp.bfloat16)
    lo = (value - hi.astype(jnp.float32)).astype(jnp.bfloat16)
    return hi, lo


def local(
    features,
    first_weight,
    second_weight,
    tile_rows,
    tile_cols,
    tile_live,
    column_mask,
    edge_weight,
    cotangent,
):
    f32 = jnp.float32
    bf16 = jnp.bfloat16
    n_rows_axis = lax.axis_size("row")
    n_cols_axis = lax.axis_size("col")
    node_count = features.shape[0]
    row_groups = n_cols_axis * node_count // BLOCK
    col_groups = n_rows_axis * node_count // BLOCK

    live = tile_live.reshape(1)
    rows = tile_rows[0, 0]
    cols = tile_cols[0, 0]
    tiles = edge_weight[0, 0]
    mask = column_mask[0, 0].astype(f32)[:, None, :]

    x_panel = gather_blocks(features, "row")
    partial_in, partial_deg = forward_aggregate(
        live, rows, cols, tiles, mask, x_panel, row_groups, with_degree=True
    )
    deg_hi, deg_lo = split_hi_lo(partial_deg[:, 0, :])
    shared = jnp.concatenate([deg_hi, deg_lo, cotangent], axis=0)
    packed = jnp.concatenate(
        [partial_in, jnp.broadcast_to(shared[None], (row_groups,) + shared.shape)], axis=1
    )
    arrived = scatter_blocks(packed, "col")
    summed_in = jnp.sum(arrived[:, :BLOCK].astype(f32), axis=0)
    degrees = jnp.sum(arrived[:, BLOCK : BLOCK + 2 * row_groups].astype(f32), axis=0)
    degrees = degrees[:row_groups] + degrees[row_groups:]
    group_cot = arrived[:, BLOCK + 2 * row_groups :]
    group_scale = 1.0 / jnp.sqrt(1.0 + degrees)
    me = lax.axis_index("col")
    row_scale = lax.dynamic_index_in_dim(group_scale, me, axis=0, keepdims=False)[:, None]

    first_mix = (features.astype(f32) + row_scale * summed_in).astype(bf16)
    first_pre = jnp.dot(first_mix, first_weight, preferred_element_type=f32)
    hidden = gelu_tanh(first_pre).astype(bf16)
    projected = jnp.dot(hidden, second_weight, preferred_element_type=f32)

    grad_panel_t = jnp.swapaxes(
        (group_scale[:, :, None] * group_cot.astype(f32)).astype(bf16), 1, 2
    )
    partial_back_t = transpose_aggregate(live, rows, cols, tiles, mask, grad_panel_t, col_groups)

    packed = jnp.concatenate(
        [jnp.broadcast_to(projected.astype(bf16)[None], (col_groups, BLOCK, BLOCK)), partial_back_t],
        axis=1,
    )
    arrived = scatter_blocks(packed, "row")
    y_panel = arrived[:, :BLOCK]
    returned_t = jnp.sum(arrived[:, BLOCK:].astype(f32), axis=0)
    (partial_y,) = forward_aggregate(live, rows, cols, tiles, mask, y_panel, row_groups, with_degree=False)

    hp = lax.Precision.HIGHEST
    combined = cotangent.astype(f32) + returned_t.T
    hidden_grad = jnp.dot(combined, second_weight.astype(f32).T, precision=hp, preferred_element_type=f32)
    pre_grad = (hidden_grad * gelu_slope(first_pre)).astype(bf16)
    first_term = jnp.dot(first_mix.T, pre_grad, preferred_element_type=f32)
    second_term = jnp.dot(hidden.astype(f32).T, combined, precision=hp, preferred_element_type=f32)
    node_scale = 1.0 / math.sqrt(node_count * n_rows_axis * n_cols_axis)
    flat = jnp.concatenate([first_term.reshape(-1), second_term.reshape(-1)]) * node_scale
    slices = flat.reshape(row_groups, -1, BLOCK)
    slice_rows = slices.shape[1]
    grad_hi, grad_lo = split_hi_lo(slices)

    packed = jnp.concatenate([partial_y, grad_hi, grad_lo], axis=1)
    arrived = scatter_blocks(packed, "col").astype(f32)
    summed_y = jnp.sum(arrived[:, :BLOCK], axis=0)
    output = (projected + row_scale * summed_y).astype(bf16)
    part = jnp.sum(arrived[:, BLOCK:], axis=0)
    part = part[:slice_rows] + part[slice_rows:]

    total = jnp.sum(gather_blocks(part, "row"), axis=0)
    everything = gather_blocks(total, "col").reshape(-1)
    split = first_term.size
    first_grad = everything[:split].reshape(first_term.shape)
    second_grad = everything[split:].reshape(second_term.shape)
    return (output, first_grad, second_grad)


def solution(mesh):
    return jax.shard_map(
        local,
        mesh=mesh,
        in_specs=(
            P(("row", "col"), None),
            P(),
            P(),
            P("row", "col", None),
            P("row", "col", None),
            P("row", "col"),
            P("row", "col", None, None),
            P("row", "col", None, None, None),
            P(("row", "col"), None),
        ),
        out_specs=(P(("row", "col"), None), P(), P()),
        check_vma=False,
    )
```

```python
import functools
import math

import jax
import jax.numpy as jnp
from jax import lax
from jax.experimental import pallas as pl
from jax.experimental.pallas import tpu as pltpu
from jax.sharding import PartitionSpec as P

BLOCK = 128


gelu_coef = math.sqrt(2.0 / math.pi)


def gelu_tanh(value):
    return 0.5 * value * (1.0 + jnp.tanh(gelu_coef * (value + 0.044715 * value * value * value)))


def gelu_slope(value):
    tanh_value = jnp.tanh(gelu_coef * (value + 0.044715 * value * value * value))
    return 0.5 * (1.0 + tanh_value) + 0.5 * value * (1.0 - tanh_value * tanh_value) * gelu_coef * (
        1.0 + 3.0 * 0.044715 * value * value
    )


UNROLL = 8


def _slot(k, u, n_live, slots):
    index = k * UNROLL + u
    return jnp.minimum(index, slots - 1), (index < n_live).astype(jnp.float32)


def _masked_tile(tiles_ref, mask_ref, s, keep):
    return (tiles_ref[s].astype(jnp.float32) * (mask_ref[s] * keep)).astype(jnp.bfloat16)


def _forward_kernel(with_degree, live_ref, rows_ref, cols_ref, tiles_ref, mask_ref, src_ref, *rest):
    if with_degree:
        out_ref, deg_ref, acc_ref, dacc_ref = rest
    else:
        out_ref, acc_ref = rest
    slots = tiles_ref.shape[0]
    n_dst = acc_ref.shape[0]
    n_src = src_ref.shape[0]
    acc_ref[...] = jnp.zeros_like(acc_ref)
    if with_degree:
        dacc_ref[...] = jnp.zeros_like(dacc_ref)
    ones = jnp.ones((8, BLOCK), jnp.bfloat16)
    n_live = jnp.clip(live_ref[0], 0, slots)

    def body(k, carry):
        for u in range(UNROLL):
            s, keep = _slot(k, u, n_live, slots)
            r = jnp.clip(rows_ref[s], 0, n_dst - 1)
            c = jnp.clip(cols_ref[s], 0, n_src - 1)
            tile = _masked_tile(tiles_ref, mask_ref, s, keep)
            acc_ref[r] += jnp.dot(tile, src_ref[c], preferred_element_type=jnp.float32)
            if with_degree:
                dacc_ref[r] += lax.dot_general(
                    ones, tile, (((1,), (1,)), ((), ())), preferred_element_type=jnp.float32
                )
        return carry

    lax.fori_loop(0, (n_live + UNROLL - 1) // UNROLL, body, 0)
    out_ref[...] = acc_ref[...].astype(out_ref.dtype)
    if with_degree:
        deg_ref[...] = dacc_ref[...]


def _transpose_kernel(live_ref, rows_ref, cols_ref, tiles_ref, mask_ref, src_ref, out_ref, acc_ref):
    slots = tiles_ref.shape[0]
    n_dst = acc_ref.shape[0]
    n_src = src_ref.shape[0]
    acc_ref[...] = jnp.zeros_like(acc_ref)
    n_live = jnp.clip(live_ref[0], 0, slots)

    def body(k, carry):
        for u in range(UNROLL):
            s, keep = _slot(k, u, n_live, slots)
            r = jnp.clip(rows_ref[s], 0, n_src - 1)
            c = jnp.clip(cols_ref[s], 0, n_dst - 1)
            tile = _masked_tile(tiles_ref, mask_ref, s, keep)
            acc_ref[c] += jnp.dot(src_ref[r], tile, preferred_element_type=jnp.float32)
        return carry

    lax.fori_loop(0, (n_live + UNROLL - 1) // UNROLL, body, 0)
    out_ref[...] = acc_ref[...].astype(out_ref.dtype)


_SMEM = pl.BlockSpec(memory_space=pltpu.SMEM)
_VMEM = pl.BlockSpec(memory_space=pltpu.VMEM)


def forward_aggregate(live, rows, cols, tiles, mask, src, n_dst, with_degree):
    width = src.shape[-1]
    slots = tiles.shape[0]
    out_shape = [jax.ShapeDtypeStruct((n_dst, BLOCK, width), jnp.bfloat16)]
    scratch = [pltpu.VMEM((n_dst, BLOCK, width), jnp.float32)]
    if with_degree:
        out_shape.append(jax.ShapeDtypeStruct((n_dst, 8, BLOCK), jnp.float32))
        scratch.append(pltpu.VMEM((n_dst, 8, BLOCK), jnp.float32))
    flops = 2 * slots * BLOCK * BLOCK * (width + (8 if with_degree else 0))
    bytes_accessed = tiles.size * 2 + src.size * 2 + n_dst * BLOCK * width * 2
    return pl.pallas_call(
        functools.partial(_forward_kernel, with_degree),
        out_shape=tuple(out_shape),
        in_specs=[_SMEM, _SMEM, _SMEM, _VMEM, _VMEM, _VMEM],
        out_specs=tuple([_VMEM] * len(out_shape)),
        scratch_shapes=scratch,
        cost_estimate=pl.CostEstimate(flops=flops, bytes_accessed=bytes_accessed, transcendentals=0),
    )(live, rows, cols, tiles, mask, src)


def transpose_aggregate(live, rows, cols, tiles, mask, src_t, n_dst):
    width = src_t.shape[1]
    slots = tiles.shape[0]
    flops = 2 * slots * BLOCK * BLOCK * width
    bytes_accessed = tiles.size * 2 + src_t.size * 2 + n_dst * BLOCK * width * 2
    return pl.pallas_call(
        _transpose_kernel,
        out_shape=jax.ShapeDtypeStruct((n_dst, width, BLOCK), jnp.bfloat16),
        in_specs=[_SMEM, _SMEM, _SMEM, _VMEM, _VMEM, _VMEM],
        out_specs=_VMEM,
        scratch_shapes=[pltpu.VMEM((n_dst, width, BLOCK), jnp.float32)],
        cost_estimate=pl.CostEstimate(flops=flops, bytes_accessed=bytes_accessed, transcendentals=0),
    )(live, rows, cols, tiles, mask, src_t)


def gather_blocks(block, axis):
    n = lax.axis_size(axis)
    return lax.all_to_all(jnp.broadcast_to(block[None], (n,) + block.shape), axis, 0, 0, tiled=False)


def scatter_blocks(blocks, axis):
    return lax.all_to_all(blocks, axis, 0, 0, tiled=False)


def split_hi_lo(value):
    hi = value.astype(jnp.bfloat16)
    lo = (value - hi.astype(jnp.float32)).astype(jnp.bfloat16)
    return hi, lo


def local(
    features,
    first_weight,
    second_weight,
    tile_rows,
    tile_cols,
    tile_live,
    column_mask,
    edge_weight,
    cotangent,
):
    f32 = jnp.float32
    bf16 = jnp.bfloat16
    n_rows_axis = lax.axis_size("row")
    n_cols_axis = lax.axis_size("col")
    node_count = features.shape[0]
    row_groups = n_cols_axis * node_count // BLOCK
    col_groups = n_rows_axis * node_count // BLOCK

    live = tile_live.reshape(1)
    rows = tile_rows[0, 0]
    cols = tile_cols[0, 0]
    tiles = edge_weight[0, 0]
    mask = column_mask[0, 0].astype(f32)[:, None, :]

    x_panel = gather_blocks(features, "row")
    partial_in, partial_deg = forward_aggregate(
        live, rows, cols, tiles, mask, x_panel, row_groups, with_degree=True
    )
    deg_hi, deg_lo = split_hi_lo(partial_deg[:, 0, :])
    shared = jnp.concatenate([deg_hi, deg_lo, cotangent], axis=0)
    packed = jnp.concatenate(
        [partial_in, jnp.broadcast_to(shared[None], (row_groups,) + shared.shape)], axis=1
    )
    arrived = scatter_blocks(packed, "col")
    summed_in = jnp.sum(arrived[:, :BLOCK].astype(f32), axis=0)
    degrees = jnp.sum(arrived[:, BLOCK : BLOCK + 2 * row_groups].astype(f32), axis=0)
    degrees = degrees[:row_groups] + degrees[row_groups:]
    group_cot = arrived[:, BLOCK + 2 * row_groups :]
    group_scale = 1.0 / jnp.sqrt(1.0 + degrees)
    me = lax.axis_index("col")
    row_scale = lax.dynamic_index_in_dim(group_scale, me, axis=0, keepdims=False)[:, None]

    first_mix = (features.astype(f32) + row_scale * summed_in).astype(bf16)
    first_pre = jnp.dot(first_mix, first_weight, preferred_element_type=f32)
    hidden = gelu_tanh(first_pre).astype(bf16)
    projected = jnp.dot(hidden, second_weight, preferred_element_type=f32)

    grad_panel_t = jnp.swapaxes(
        (group_scale[:, :, None] * group_cot.astype(f32)).astype(bf16), 1, 2
    )
    partial_back_t = transpose_aggregate(live, rows, cols, tiles, mask, grad_panel_t, col_groups)

    packed = jnp.concatenate(
        [jnp.broadcast_to(projected.astype(bf16)[None], (col_groups, BLOCK, BLOCK)), partial_back_t],
        axis=1,
    )
    arrived = scatter_blocks(packed, "row")
    y_panel = arrived[:, :BLOCK]
    returned_t = jnp.sum(arrived[:, BLOCK:].astype(f32), axis=0)
    (partial_y,) = forward_aggregate(live, rows, cols, tiles, mask, y_panel, row_groups, with_degree=False)

    hp = lax.Precision.HIGHEST
    combined = cotangent.astype(f32) + returned_t.T
    hidden_grad = jnp.dot(combined, second_weight.astype(f32).T, precision=hp, preferred_element_type=f32)
    pre_grad = (hidden_grad * gelu_slope(first_pre)).astype(bf16)
    first_term = jnp.dot(first_mix.T, pre_grad, preferred_element_type=f32)
    second_term = jnp.dot(hidden.astype(f32).T, combined, precision=hp, preferred_element_type=f32)
    node_scale = 1.0 / math.sqrt(node_count * n_rows_axis * n_cols_axis)
    flat = jnp.concatenate([first_term.reshape(-1), second_term.reshape(-1)]) * node_scale
    slices = flat.reshape(row_groups, -1, BLOCK)
    slice_rows = slices.shape[1]
    grad_hi, grad_lo = split_hi_lo(slices)

    packed = jnp.concatenate([partial_y, grad_hi, grad_lo], axis=1)
    arrived = scatter_blocks(packed, "col").astype(f32)
    summed_y = jnp.sum(arrived[:, :BLOCK], axis=0)
    output = (projected + row_scale * summed_y).astype(bf16)
    part = jnp.sum(arrived[:, BLOCK:], axis=0)
    part = part[:slice_rows] + part[slice_rows:]

    total = jnp.sum(gather_blocks(part, "row"), axis=0)
    everything = gather_blocks(total, "col").reshape(-1)
    split = first_term.size
    first_grad = everything[:split].reshape(first_term.shape)
    second_grad = everything[split:].reshape(second_term.shape)
    return (output, first_grad, second_grad)


def solution(mesh):
    return jax.shard_map(
        local,
        mesh=mesh,
        in_specs=(
            P(("row", "col"), None),
            P(),
            P(),
            P("row", "col", None),
            P("row", "col", None),
            P("row", "col"),
            P("row", "col", None, None),
            P("row", "col", None, None, None),
            P(("row", "col"), None),
        ),
        out_specs=(P(("row", "col"), None), P(), P()),
        check_vma=False,
    )
```

```python
import functools
import math

import jax
import jax.numpy as jnp
from jax import lax
from jax.experimental import pallas as pl
from jax.experimental.pallas import tpu as pltpu
from jax.sharding import PartitionSpec as P

BLOCK = 128


gelu_coef = math.sqrt(2.0 / math.pi)


def gelu_tanh(value):
    return 0.5 * value * (1.0 + jnp.tanh(gelu_coef * (value + 0.044715 * value * value * value)))


def gelu_slope(value):
    tanh_value = jnp.tanh(gelu_coef * (value + 0.044715 * value * value * value))
    return 0.5 * (1.0 + tanh_value) + 0.5 * value * (1.0 - tanh_value * tanh_value) * gelu_coef * (
        1.0 + 3.0 * 0.044715 * value * value
    )


UNROLL = 16


def _slot(k, u, n_live, slots):
    index = k * UNROLL + u
    return jnp.minimum(index, slots - 1), (index < n_live).astype(jnp.float32)


def _masked_tile(tiles_ref, mask_ref, s, keep):
    return (tiles_ref[s].astype(jnp.float32) * (mask_ref[s] * keep)).astype(jnp.bfloat16)


def _forward_kernel(with_degree, live_ref, rows_ref, cols_ref, tiles_ref, mask_ref, src_ref, *rest):
    if with_degree:
        out_ref, deg_ref, acc_ref, dacc_ref = rest
    else:
        out_ref, acc_ref = rest
    slots = tiles_ref.shape[0]
    n_dst = acc_ref.shape[0]
    n_src = src_ref.shape[0]
    acc_ref[...] = jnp.zeros_like(acc_ref)
    if with_degree:
        dacc_ref[...] = jnp.zeros_like(dacc_ref)
    ones = jnp.ones((8, BLOCK), jnp.bfloat16)
    n_live = jnp.clip(live_ref[0], 0, slots)

    def body(k, carry):
        for u in range(UNROLL):
            s, keep = _slot(k, u, n_live, slots)
            r = jnp.clip(rows_ref[s], 0, n_dst - 1)
            c = jnp.clip(cols_ref[s], 0, n_src - 1)
            tile = _masked_tile(tiles_ref, mask_ref, s, keep)
            acc_ref[r] += jnp.dot(tile, src_ref[c], preferred_element_type=jnp.float32)
            if with_degree:
                dacc_ref[r] += lax.dot_general(
                    ones, tile, (((1,), (1,)), ((), ())), preferred_element_type=jnp.float32
                )
        return carry

    lax.fori_loop(0, (n_live + UNROLL - 1) // UNROLL, body, 0)
    out_ref[...] = acc_ref[...].astype(out_ref.dtype)
    if with_degree:
        deg_ref[...] = dacc_ref[...]


def _transpose_kernel(live_ref, rows_ref, cols_ref, tiles_ref, mask_ref, src_ref, out_ref, acc_ref):
    slots = tiles_ref.shape[0]
    n_dst = acc_ref.shape[0]
    n_src = src_ref.shape[0]
    acc_ref[...] = jnp.zeros_like(acc_ref)
    n_live = jnp.clip(live_ref[0], 0, slots)

    def body(k, carry):
        for u in range(UNROLL):
            s, keep = _slot(k, u, n_live, slots)
            r = jnp.clip(rows_ref[s], 0, n_src - 1)
            c = jnp.clip(cols_ref[s], 0, n_dst - 1)
            tile = _masked_tile(tiles_ref, mask_ref, s, keep)
            acc_ref[c] += jnp.dot(src_ref[r], tile, preferred_element_type=jnp.float32)
        return carry

    lax.fori_loop(0, (n_live + UNROLL - 1) // UNROLL, body, 0)
    out_ref[...] = acc_ref[...].astype(out_ref.dtype)


_SMEM = pl.BlockSpec(memory_space=pltpu.SMEM)
_VMEM = pl.BlockSpec(memory_space=pltpu.VMEM)


def forward_aggregate(live, rows, cols, tiles, mask, src, n_dst, with_degree):
    width = src.shape[-1]
    slots = tiles.shape[0]
    out_shape = [jax.ShapeDtypeStruct((n_dst, BLOCK, width), jnp.bfloat16)]
    scratch = [pltpu.VMEM((n_dst, BLOCK, width), jnp.float32)]
    if with_degree:
        out_shape.append(jax.ShapeDtypeStruct((n_dst, 8, BLOCK), jnp.float32))
        scratch.append(pltpu.VMEM((n_dst, 8, BLOCK), jnp.float32))
    flops = 2 * slots * BLOCK * BLOCK * (width + (8 if with_degree else 0))
    bytes_accessed = tiles.size * 2 + src.size * 2 + n_dst * BLOCK * width * 2
    return pl.pallas_call(
        functools.partial(_forward_kernel, with_degree),
        out_shape=tuple(out_shape),
        in_specs=[_SMEM, _SMEM, _SMEM, _VMEM, _VMEM, _VMEM],
        out_specs=tuple([_VMEM] * len(out_shape)),
        scratch_shapes=scratch,
        cost_estimate=pl.CostEstimate(flops=flops, bytes_accessed=bytes_accessed, transcendentals=0),
    )(live, rows, cols, tiles, mask, src)


def transpose_aggregate(live, rows, cols, tiles, mask, src_t, n_dst):
    width = src_t.shape[1]
    slots = tiles.shape[0]
    flops = 2 * slots * BLOCK * BLOCK * width
    bytes_accessed = tiles.size * 2 + src_t.size * 2 + n_dst * BLOCK * width * 2
    return pl.pallas_call(
        _transpose_kernel,
        out_shape=jax.ShapeDtypeStruct((n_dst, width, BLOCK), jnp.bfloat16),
        in_specs=[_SMEM, _SMEM, _SMEM, _VMEM, _VMEM, _VMEM],
        out_specs=_VMEM,
        scratch_shapes=[pltpu.VMEM((n_dst, width, BLOCK), jnp.float32)],
        cost_estimate=pl.CostEstimate(flops=flops, bytes_accessed=bytes_accessed, transcendentals=0),
    )(live, rows, cols, tiles, mask, src_t)


def gather_blocks(block, axis):
    n = lax.axis_size(axis)
    return lax.all_to_all(jnp.broadcast_to(block[None], (n,) + block.shape), axis, 0, 0, tiled=False)


def scatter_blocks(blocks, axis):
    return lax.all_to_all(blocks, axis, 0, 0, tiled=False)


def split_hi_lo(value):
    hi = value.astype(jnp.bfloat16)
    lo = (value - hi.astype(jnp.float32)).astype(jnp.bfloat16)
    return hi, lo


def local(
    features,
    first_weight,
    second_weight,
    tile_rows,
    tile_cols,
    tile_live,
    column_mask,
    edge_weight,
    cotangent,
):
    f32 = jnp.float32
    bf16 = jnp.bfloat16
    n_rows_axis = lax.axis_size("row")
    n_cols_axis = lax.axis_size("col")
    node_count = features.shape[0]
    row_groups = n_cols_axis * node_count // BLOCK
    col_groups = n_rows_axis * node_count // BLOCK

    live = tile_live.reshape(1)
    rows = tile_rows[0, 0]
    cols = tile_cols[0, 0]
    tiles = edge_weight[0, 0]
    mask = column_mask[0, 0].astype(f32)[:, None, :]

    x_panel = gather_blocks(features, "row")
    partial_in, partial_deg = forward_aggregate(
        live, rows, cols, tiles, mask, x_panel, row_groups, with_degree=True
    )
    shared = jnp.concatenate([partial_deg[:, 0, :].astype(bf16), cotangent], axis=0)
    packed = jnp.concatenate(
        [partial_in, jnp.broadcast_to(shared[None], (row_groups,) + shared.shape)], axis=1
    )
    arrived = scatter_blocks(packed, "col")
    summed_in = jnp.sum(arrived[:, :BLOCK].astype(f32), axis=0)
    degrees = jnp.sum(arrived[:, BLOCK : BLOCK + row_groups].astype(f32), axis=0)
    group_cot = arrived[:, BLOCK + row_groups :]
    group_scale = 1.0 / jnp.sqrt(1.0 + degrees)
    me = lax.axis_index("col")
    row_scale = lax.dynamic_index_in_dim(group_scale, me, axis=0, keepdims=False)[:, None]

    first_mix = (features.astype(f32) + row_scale * summed_in).astype(bf16)
    first_pre = jnp.dot(first_mix, first_weight, preferred_element_type=f32)
    hidden = gelu_tanh(first_pre).astype(bf16)
    projected = jnp.dot(hidden, second_weight, preferred_element_type=f32)

    grad_panel_t = jnp.swapaxes(
        (group_scale[:, :, None] * group_cot.astype(f32)).astype(bf16), 1, 2
    )
    partial_back_t = transpose_aggregate(live, rows, cols, tiles, mask, grad_panel_t, col_groups)

    packed = jnp.concatenate(
        [jnp.broadcast_to(projected.astype(bf16)[None], (col_groups, BLOCK, BLOCK)), partial_back_t],
        axis=1,
    )
    arrived = scatter_blocks(packed, "row")
    y_panel = arrived[:, :BLOCK]
    returned_t = jnp.sum(arrived[:, BLOCK:].astype(f32), axis=0)
    (partial_y,) = forward_aggregate(live, rows, cols, tiles, mask, y_panel, row_groups, with_degree=False)

    hp = lax.Precision.HIGHEST
    combined = cotangent.astype(f32) + returned_t.T
    hidden_grad = jnp.dot(combined, second_weight.astype(f32).T, precision=hp, preferred_element_type=f32)
    pre_grad = (hidden_grad * gelu_slope(first_pre)).astype(bf16)
    first_term = jnp.dot(first_mix.T, pre_grad, preferred_element_type=f32)
    second_term = jnp.dot(hidden.astype(f32).T, combined, precision=hp, preferred_element_type=f32)
    node_scale = 1.0 / math.sqrt(node_count * n_rows_axis * n_cols_axis)
    flat = jnp.concatenate([first_term.reshape(-1), second_term.reshape(-1)]) * node_scale
    slices = flat.reshape(row_groups, -1, BLOCK)

    packed = jnp.concatenate([partial_y, slices.astype(bf16)], axis=1)
    arrived = scatter_blocks(packed, "col").astype(f32)
    summed_y = jnp.sum(arrived[:, :BLOCK], axis=0)
    output = (projected + row_scale * summed_y).astype(bf16)
    part = jnp.sum(arrived[:, BLOCK:], axis=0)

    total = jnp.sum(gather_blocks(part.astype(bf16), "row").astype(f32), axis=0)
    everything = gather_blocks(total.astype(bf16), "col").astype(f32).reshape(-1)
    split = first_term.size
    first_grad = everything[:split].reshape(first_term.shape)
    second_grad = everything[split:].reshape(second_term.shape)
    return (output, first_grad, second_grad)


def solution(mesh):
    return jax.shard_map(
        local,
        mesh=mesh,
        in_specs=(
            P(("row", "col"), None),
            P(),
            P(),
            P("row", "col", None),
            P("row", "col", None),
            P("row", "col"),
            P("row", "col", None, None),
            P("row", "col", None, None, None),
            P(("row", "col"), None),
        ),
        out_specs=(P(("row", "col"), None), P(), P()),
        check_vma=False,
    )
```

```python
import functools
import math

import jax
import jax.numpy as jnp
from jax import lax
from jax.experimental import pallas as pl
from jax.experimental.pallas import tpu as pltpu
from jax.sharding import PartitionSpec as P

BLOCK = 128


gelu_coef = math.sqrt(2.0 / math.pi)


def gelu_tanh(value):
    return 0.5 * value * (1.0 + jnp.tanh(gelu_coef * (value + 0.044715 * value * value * value)))


def gelu_slope(value):
    tanh_value = jnp.tanh(gelu_coef * (value + 0.044715 * value * value * value))
    return 0.5 * (1.0 + tanh_value) + 0.5 * value * (1.0 - tanh_value * tanh_value) * gelu_coef * (
        1.0 + 3.0 * 0.044715 * value * value
    )


UNROLL = 16


def _slot(k, u, n_live, slots):
    index = k * UNROLL + u
    return jnp.minimum(index, slots - 1), (index < n_live).astype(jnp.float32)


def _masked_tile(tiles_ref, mask_ref, s, keep):
    return (tiles_ref[s].astype(jnp.float32) * (mask_ref[s] * keep)).astype(jnp.bfloat16)


def _forward_kernel(row_offset, live_ref, rows_ref, cols_ref, tiles_ref, mask_ref, src_ref, into_ref, out_ref,
                    acc_ref, stage_ref, sem):
    del into_ref
    slots = tiles_ref.shape[0]
    n_dst = acc_ref.shape[0]
    n_src = src_ref.shape[0]
    acc_ref[...] = jnp.zeros_like(acc_ref)
    n_live = jnp.clip(live_ref[0], 0, slots)

    def body(k, carry):
        for u in range(UNROLL):
            s, keep = _slot(k, u, n_live, slots)
            r = jnp.clip(rows_ref[s], 0, n_dst - 1)
            c = jnp.clip(cols_ref[s], 0, n_src - 1)
            tile = _masked_tile(tiles_ref, mask_ref, s, keep)
            acc_ref[r] += jnp.dot(tile, src_ref[c], preferred_element_type=jnp.float32)
        return carry

    lax.fori_loop(0, (n_live + UNROLL - 1) // UNROLL, body, 0)
    stage_ref[...] = acc_ref[...].astype(stage_ref.dtype)
    copy = pltpu.make_async_copy(stage_ref, out_ref.at[:, pl.ds(row_offset, BLOCK), :], sem)
    copy.start()
    copy.wait()


def _transpose_kernel(row_offset, live_ref, rows_ref, cols_ref, tiles_ref, mask_ref, src_ref, into_ref, out_ref,
                      acc_ref, stage_ref, sem):
    del into_ref
    slots = tiles_ref.shape[0]
    n_dst = acc_ref.shape[0]
    n_src = src_ref.shape[0]
    acc_ref[...] = jnp.zeros_like(acc_ref)
    n_live = jnp.clip(live_ref[0], 0, slots)

    def body(k, carry):
        for u in range(UNROLL):
            s, keep = _slot(k, u, n_live, slots)
            r = jnp.clip(rows_ref[s], 0, n_src - 1)
            c = jnp.clip(cols_ref[s], 0, n_dst - 1)
            tile = _masked_tile(tiles_ref, mask_ref, s, keep)
            acc_ref[c] += jnp.dot(src_ref[r], tile, preferred_element_type=jnp.float32)
        return carry

    lax.fori_loop(0, (n_live + UNROLL - 1) // UNROLL, body, 0)
    stage_ref[...] = acc_ref[...].astype(stage_ref.dtype)
    copy = pltpu.make_async_copy(stage_ref, out_ref.at[:, pl.ds(row_offset, BLOCK), :], sem)
    copy.start()
    copy.wait()


_SMEM = pl.BlockSpec(memory_space=pltpu.SMEM)
_VMEM = pl.BlockSpec(memory_space=pltpu.VMEM)
_ANY = pl.BlockSpec(memory_space=pl.ANY)


def _aggregate_into(kernel, live, rows, cols, tiles, mask, src, into, row_offset):
    n_dst = into.shape[0]
    width = into.shape[2]
    slots = tiles.shape[0]
    flops = 2 * slots * BLOCK * BLOCK * width
    bytes_accessed = tiles.size * 2 + src.size * 2 + n_dst * BLOCK * width * 2
    return pl.pallas_call(
        functools.partial(kernel, row_offset),
        out_shape=jax.ShapeDtypeStruct(into.shape, into.dtype),
        in_specs=[_SMEM, _SMEM, _SMEM, _VMEM, _VMEM, _VMEM, _ANY],
        out_specs=_ANY,
        scratch_shapes=[
            pltpu.VMEM((n_dst, BLOCK, width), jnp.float32),
            pltpu.VMEM((n_dst, BLOCK, width), into.dtype),
            pltpu.SemaphoreType.DMA(()),
        ],
        input_output_aliases={6: 0},
        cost_estimate=pl.CostEstimate(flops=flops, bytes_accessed=bytes_accessed, transcendentals=0),
    )(live, rows, cols, tiles, mask, src, into)


def forward_aggregate_into(live, rows, cols, tiles, mask, src, into, row_offset):
    return _aggregate_into(_forward_kernel, live, rows, cols, tiles, mask, src, into, row_offset)


def transpose_aggregate_into(live, rows, cols, tiles, mask, src_t, into, row_offset):
    return _aggregate_into(_transpose_kernel, live, rows, cols, tiles, mask, src_t, into, row_offset)


def gather_blocks(block, axis):
    n = lax.axis_size(axis)
    return lax.all_to_all(jnp.broadcast_to(block[None], (n,) + block.shape), axis, 0, 0, tiled=False)


def scatter_blocks(blocks, axis):
    return lax.all_to_all(blocks, axis, 0, 0, tiled=False)


def split_hi_lo(value):
    hi = value.astype(jnp.bfloat16)
    lo = (value - hi.astype(jnp.float32)).astype(jnp.bfloat16)
    return hi, lo


def local(
    features,
    first_weight,
    second_weight,
    tile_rows,
    tile_cols,
    tile_live,
    column_mask,
    edge_weight,
    cotangent,
):
    f32 = jnp.float32
    bf16 = jnp.bfloat16
    n_rows_axis = lax.axis_size("row")
    n_cols_axis = lax.axis_size("col")
    node_count = features.shape[0]
    row_groups = n_cols_axis * node_count // BLOCK
    col_groups = n_rows_axis * node_count // BLOCK

    live = tile_live.reshape(1)
    rows = tile_rows[0, 0]
    cols = tile_cols[0, 0]
    tiles = edge_weight[0, 0]
    mask = column_mask[0, 0].astype(f32)[:, None, :]

    x_panel = gather_blocks(features, "row")
    live_weight = (jnp.arange(tiles.shape[0]) < jnp.clip(live[0], 0, tiles.shape[0])).astype(f32)
    row_sums = jnp.sum(tiles.astype(f32) * mask, axis=2) * live_weight[:, None]
    partial_deg = jnp.zeros((row_groups, BLOCK), f32).at[jnp.clip(rows, 0, row_groups - 1)].add(row_sums)
    shared = jnp.concatenate([partial_deg.astype(bf16), cotangent], axis=0)
    packed = jnp.concatenate(
        [jnp.zeros((row_groups, BLOCK, BLOCK), bf16), jnp.broadcast_to(shared[None], (row_groups,) + shared.shape)],
        axis=1,
    )
    packed = forward_aggregate_into(live, rows, cols, tiles, mask, x_panel, packed, 0)
    arrived = scatter_blocks(packed, "col")
    summed_in = jnp.sum(arrived[:, :BLOCK].astype(f32), axis=0)
    degrees = jnp.sum(arrived[:, BLOCK : BLOCK + row_groups].astype(f32), axis=0)
    group_cot = arrived[:, BLOCK + row_groups :]
    group_scale = 1.0 / jnp.sqrt(1.0 + degrees)
    me = lax.axis_index("col")
    row_scale = lax.dynamic_index_in_dim(group_scale, me, axis=0, keepdims=False)[:, None]

    first_mix = (features.astype(f32) + row_scale * summed_in).astype(bf16)
    first_pre = jnp.dot(first_mix, first_weight, preferred_element_type=f32)
    hidden = gelu_tanh(first_pre).astype(bf16)
    projected = jnp.dot(hidden, second_weight, preferred_element_type=f32)

    grad_panel_t = jnp.swapaxes(
        (group_scale[:, :, None] * group_cot.astype(f32)).astype(bf16), 1, 2
    )

    packed = jnp.concatenate(
        [
            jnp.broadcast_to(projected.astype(bf16)[None], (col_groups, BLOCK, BLOCK)),
            jnp.zeros((col_groups, BLOCK, BLOCK), bf16),
        ],
        axis=1,
    )
    packed = transpose_aggregate_into(live, rows, cols, tiles, mask, grad_panel_t, packed, BLOCK)
    arrived = scatter_blocks(packed, "row")
    y_panel = arrived[:, :BLOCK]
    returned_t = jnp.sum(arrived[:, BLOCK:].astype(f32), axis=0)

    hp = lax.Precision.HIGHEST
    combined = cotangent.astype(f32) + returned_t.T
    hidden_grad = jnp.dot(combined, second_weight.astype(f32).T, precision=hp, preferred_element_type=f32)
    pre_grad = (hidden_grad * gelu_slope(first_pre)).astype(bf16)
    first_term = jnp.dot(first_mix.T, pre_grad, preferred_element_type=f32)
    second_term = jnp.dot(hidden.astype(f32).T, combined, precision=hp, preferred_element_type=f32)
    node_scale = 1.0 / math.sqrt(node_count * n_rows_axis * n_cols_axis)
    flat = jnp.concatenate([first_term.reshape(-1), second_term.reshape(-1)]) * node_scale
    slices = flat.reshape(row_groups, -1, BLOCK)

    packed = jnp.concatenate([jnp.zeros((row_groups, BLOCK, BLOCK), bf16), slices.astype(bf16)], axis=1)
    packed = forward_aggregate_into(live, rows, cols, tiles, mask, y_panel, packed, 0)
    arrived = scatter_blocks(packed, "col").astype(f32)
    summed_y = jnp.sum(arrived[:, :BLOCK], axis=0)
    output = (projected + row_scale * summed_y).astype(bf16)
    part = jnp.sum(arrived[:, BLOCK:], axis=0)

    total = jnp.sum(gather_blocks(part.astype(bf16), "row").astype(f32), axis=0)
    everything = gather_blocks(total.astype(bf16), "col").astype(f32).reshape(-1)
    split = first_term.size
    first_grad = everything[:split].reshape(first_term.shape)
    second_grad = everything[split:].reshape(second_term.shape)
    return (output, first_grad, second_grad)


def solution(mesh):
    return jax.shard_map(
        local,
        mesh=mesh,
        in_specs=(
            P(("row", "col"), None),
            P(),
            P(),
            P("row", "col", None),
            P("row", "col", None),
            P("row", "col"),
            P("row", "col", None, None),
            P("row", "col", None, None, None),
            P(("row", "col"), None),
        ),
        out_specs=(P(("row", "col"), None), P(), P()),
        check_vma=False,
    )
```

```python
import functools
import math

import jax
import jax.numpy as jnp
from jax import lax
from jax.experimental import pallas as pl
from jax.experimental.pallas import tpu as pltpu
from jax.sharding import PartitionSpec as P

BLOCK = 128


gelu_coef = math.sqrt(2.0 / math.pi)


def gelu_tanh(value):
    return 0.5 * value * (1.0 + jnp.tanh(gelu_coef * (value + 0.044715 * value * value * value)))


def gelu_slope(value):
    tanh_value = jnp.tanh(gelu_coef * (value + 0.044715 * value * value * value))
    return 0.5 * (1.0 + tanh_value) + 0.5 * value * (1.0 - tanh_value * tanh_value) * gelu_coef * (
        1.0 + 3.0 * 0.044715 * value * value
    )


UNROLL = 16


def _slot(k, u, n_live, slots):
    index = k * UNROLL + u
    return jnp.minimum(index, slots - 1), (index < n_live).astype(jnp.float32)


def _masked_tile(tiles_ref, mask_ref, s, keep):
    column = mask_ref[pl.ds(s, 1), :].astype(jnp.float32) * keep
    return (tiles_ref[s].astype(jnp.float32) * column).astype(jnp.bfloat16)


def _forward_kernel(row_offset, live_ref, rows_ref, cols_ref, tiles_ref, mask_ref, src_ref, into_ref, out_ref,
                    acc_ref, stage_ref, sem):
    del into_ref
    slots = tiles_ref.shape[0]
    n_dst = acc_ref.shape[0]
    n_src = src_ref.shape[0]
    acc_ref[...] = jnp.zeros_like(acc_ref)
    n_live = jnp.clip(live_ref[0], 0, slots)

    def body(k, carry):
        for u in range(UNROLL):
            s, keep = _slot(k, u, n_live, slots)
            r = jnp.clip(rows_ref[s], 0, n_dst - 1)
            c = jnp.clip(cols_ref[s], 0, n_src - 1)
            tile = _masked_tile(tiles_ref, mask_ref, s, keep)
            acc_ref[r] += jnp.dot(tile, src_ref[c], preferred_element_type=jnp.float32)
        return carry

    lax.fori_loop(0, (n_live + UNROLL - 1) // UNROLL, body, 0)
    stage_ref[...] = acc_ref[...].astype(stage_ref.dtype)
    copy = pltpu.make_async_copy(stage_ref, out_ref.at[:, pl.ds(row_offset, BLOCK), :], sem)
    copy.start()
    copy.wait()


def _transpose_kernel(row_offset, live_ref, rows_ref, cols_ref, tiles_ref, mask_ref, src_ref, into_ref, out_ref,
                      acc_ref, stage_ref, sem):
    del into_ref
    slots = tiles_ref.shape[0]
    n_dst = acc_ref.shape[0]
    n_src = src_ref.shape[0]
    acc_ref[...] = jnp.zeros_like(acc_ref)
    n_live = jnp.clip(live_ref[0], 0, slots)

    def body(k, carry):
        for u in range(UNROLL):
            s, keep = _slot(k, u, n_live, slots)
            r = jnp.clip(rows_ref[s], 0, n_src - 1)
            c = jnp.clip(cols_ref[s], 0, n_dst - 1)
            tile = _masked_tile(tiles_ref, mask_ref, s, keep)
            acc_ref[c] += jnp.dot(src_ref[r], tile, preferred_element_type=jnp.float32)
        return carry

    lax.fori_loop(0, (n_live + UNROLL - 1) // UNROLL, body, 0)
    stage_ref[...] = acc_ref[...].astype(stage_ref.dtype)
    copy = pltpu.make_async_copy(stage_ref, out_ref.at[:, pl.ds(row_offset, BLOCK), :], sem)
    copy.start()
    copy.wait()


_SMEM = pl.BlockSpec(memory_space=pltpu.SMEM)
_VMEM = pl.BlockSpec(memory_space=pltpu.VMEM)
_ANY = pl.BlockSpec(memory_space=pl.ANY)


def _aggregate_into(kernel, live, rows, cols, tiles, mask, src, into, row_offset):
    n_dst = into.shape[0]
    width = into.shape[2]
    slots = tiles.shape[0]
    flops = 2 * slots * BLOCK * BLOCK * width
    bytes_accessed = tiles.size * 2 + src.size * 2 + n_dst * BLOCK * width * 2
    return pl.pallas_call(
        functools.partial(kernel, row_offset),
        out_shape=jax.ShapeDtypeStruct(into.shape, into.dtype),
        in_specs=[_SMEM, _SMEM, _SMEM, _VMEM, _VMEM, _VMEM, _ANY],
        out_specs=_ANY,
        scratch_shapes=[
            pltpu.VMEM((n_dst, BLOCK, width), jnp.float32),
            pltpu.VMEM((n_dst, BLOCK, width), into.dtype),
            pltpu.SemaphoreType.DMA(()),
        ],
        input_output_aliases={6: 0},
        cost_estimate=pl.CostEstimate(flops=flops, bytes_accessed=bytes_accessed, transcendentals=0),
    )(live, rows, cols, tiles, mask, src, into)


def forward_aggregate_into(live, rows, cols, tiles, mask, src, into, row_offset):
    return _aggregate_into(_forward_kernel, live, rows, cols, tiles, mask, src, into, row_offset)


def transpose_aggregate_into(live, rows, cols, tiles, mask, src_t, into, row_offset):
    return _aggregate_into(_transpose_kernel, live, rows, cols, tiles, mask, src_t, into, row_offset)


def gather_blocks(block, axis):
    n = lax.axis_size(axis)
    return lax.all_to_all(jnp.broadcast_to(block[None], (n,) + block.shape), axis, 0, 0, tiled=False)


def scatter_blocks(blocks, axis):
    return lax.all_to_all(blocks, axis, 0, 0, tiled=False)


def split_hi_lo(value):
    hi = value.astype(jnp.bfloat16)
    lo = (value - hi.astype(jnp.float32)).astype(jnp.bfloat16)
    return hi, lo


def local(
    features,
    first_weight,
    second_weight,
    tile_rows,
    tile_cols,
    tile_live,
    column_mask,
    edge_weight,
    cotangent,
):
    f32 = jnp.float32
    bf16 = jnp.bfloat16
    n_rows_axis = lax.axis_size("row")
    n_cols_axis = lax.axis_size("col")
    node_count = features.shape[0]
    row_groups = n_cols_axis * node_count // BLOCK
    col_groups = n_rows_axis * node_count // BLOCK

    live = tile_live.reshape(1)
    rows = tile_rows[0, 0]
    cols = tile_cols[0, 0]
    tiles = edge_weight[0, 0]
    mask = column_mask[0, 0]

    x_panel = gather_blocks(features, "row")
    live_weight = (jnp.arange(tiles.shape[0]) < jnp.clip(live[0], 0, tiles.shape[0])).astype(jnp.int32)
    live_mask = (mask * live_weight[:, None]).astype(bf16)
    row_sums = jnp.einsum("sij,sj->si", tiles, live_mask, preferred_element_type=f32)
    partial_deg = jnp.zeros((row_groups, BLOCK), f32).at[jnp.clip(rows, 0, row_groups - 1)].add(row_sums)
    shared = jnp.concatenate([partial_deg.astype(bf16), cotangent.T], axis=0)
    packed = jnp.concatenate(
        [jnp.zeros((row_groups, BLOCK, BLOCK), bf16), jnp.broadcast_to(shared[None], (row_groups,) + shared.shape)],
        axis=1,
    )
    packed = forward_aggregate_into(live, rows, cols, tiles, mask, x_panel, packed, 0)
    arrived = scatter_blocks(packed, "col")
    summed_in = jnp.sum(arrived[:, :BLOCK].astype(f32), axis=0)
    degrees = jnp.sum(arrived[:, BLOCK : BLOCK + row_groups].astype(f32), axis=0)
    group_cot_t = arrived[:, BLOCK + row_groups :]
    group_scale = 1.0 / jnp.sqrt(1.0 + degrees)
    me = lax.axis_index("col")
    row_scale = lax.dynamic_index_in_dim(group_scale, me, axis=0, keepdims=False)[:, None]

    first_mix = (features.astype(f32) + row_scale * summed_in).astype(bf16)
    first_pre = jnp.dot(first_mix, first_weight, preferred_element_type=f32)
    hidden = gelu_tanh(first_pre).astype(bf16)
    projected = jnp.dot(hidden, second_weight, preferred_element_type=f32)

    grad_panel_t = (group_scale[:, None, :] * group_cot_t.astype(f32)).astype(bf16)
    packed = jnp.concatenate(
        [
            jnp.broadcast_to(projected.astype(bf16)[None], (col_groups, BLOCK, BLOCK)),
            jnp.zeros((col_groups, BLOCK, BLOCK), bf16),
        ],
        axis=1,
    )
    packed = transpose_aggregate_into(live, rows, cols, tiles, mask, grad_panel_t, packed, BLOCK)
    arrived = scatter_blocks(packed, "row")
    y_panel = arrived[:, :BLOCK]
    returned_t = jnp.sum(arrived[:, BLOCK:].astype(f32), axis=0)

    hp = lax.Precision.HIGHEST
    combined = cotangent.astype(f32) + returned_t.T
    hidden_grad = jnp.dot(combined, second_weight.astype(f32).T, precision=hp, preferred_element_type=f32)
    pre_grad = (hidden_grad * gelu_slope(first_pre)).astype(bf16)
    first_term = jnp.dot(first_mix.T, pre_grad, preferred_element_type=f32)
    second_term = jnp.dot(hidden.astype(f32).T, combined, precision=hp, preferred_element_type=f32)
    node_scale = 1.0 / math.sqrt(node_count * n_rows_axis * n_cols_axis)
    flat = jnp.concatenate([first_term.reshape(-1), second_term.reshape(-1)]) * node_scale
    slices = flat.reshape(row_groups, -1, BLOCK)

    packed = jnp.concatenate([jnp.zeros((row_groups, BLOCK, BLOCK), bf16), slices.astype(bf16)], axis=1)
    packed = forward_aggregate_into(live, rows, cols, tiles, mask, y_panel, packed, 0)
    arrived = scatter_blocks(packed, "col").astype(f32)
    summed_y = jnp.sum(arrived[:, :BLOCK], axis=0)
    output = (projected + row_scale * summed_y).astype(bf16)
    part = jnp.sum(arrived[:, BLOCK:], axis=0)

    total = jnp.sum(gather_blocks(part.astype(bf16), "row").astype(f32), axis=0)
    everything = gather_blocks(total.astype(bf16), "col").astype(f32).reshape(-1)
    split = first_term.size
    first_grad = everything[:split].reshape(first_term.shape)
    second_grad = everything[split:].reshape(second_term.shape)
    return (output, first_grad, second_grad)


def solution(mesh):
    return jax.shard_map(
        local,
        mesh=mesh,
        in_specs=(
            P(("row", "col"), None),
            P(),
            P(),
            P("row", "col", None),
            P("row", "col", None),
            P("row", "col"),
            P("row", "col", None, None),
            P("row", "col", None, None, None),
            P(("row", "col"), None),
        ),
        out_specs=(P(("row", "col"), None), P(), P()),
        check_vma=False,
    )
```

```python
import functools
import math

import jax
import jax.numpy as jnp
from jax import lax
from jax.experimental import pallas as pl
from jax.experimental.pallas import tpu as pltpu
from jax.sharding import PartitionSpec as P

BLOCK = 128


gelu_coef = math.sqrt(2.0 / math.pi)


def gelu_tanh(value):
    return 0.5 * value * (1.0 + jnp.tanh(gelu_coef * (value + 0.044715 * value * value * value)))


def gelu_slope(value):
    tanh_value = jnp.tanh(gelu_coef * (value + 0.044715 * value * value * value))
    return 0.5 * (1.0 + tanh_value) + 0.5 * value * (1.0 - tanh_value * tanh_value) * gelu_coef * (
        1.0 + 3.0 * 0.044715 * value * value
    )


UNROLL = 16


def _slot(k, u, n_live, slots):
    index = k * UNROLL + u
    return jnp.minimum(index, slots - 1), (index < n_live).astype(jnp.float32)


def _masked_tile(tiles_ref, mask_ref, s, keep):
    column = mask_ref[pl.ds(s, 1), :].astype(jnp.float32) * keep
    return (tiles_ref[s].astype(jnp.float32) * column).astype(jnp.bfloat16)


_SMEM = pl.BlockSpec(memory_space=pltpu.SMEM)
_VMEM = pl.BlockSpec(memory_space=pltpu.VMEM)
_ANY = pl.BlockSpec(memory_space=pl.ANY)


def _forward_kernel(row_offset, live_ref, rows_ref, cols_ref, tiles_ref, mask_ref, src_ref, into_ref, out_ref,
                    acc_ref, stage_ref, sem):
    del into_ref
    slots = tiles_ref.shape[0]
    n_dst = acc_ref.shape[0]
    n_src = src_ref.shape[0]
    acc_ref[...] = jnp.zeros_like(acc_ref)
    n_live = jnp.clip(live_ref[0], 0, slots)

    def body(k, carry):
        for u in range(UNROLL):
            s, keep = _slot(k, u, n_live, slots)
            r = jnp.clip(rows_ref[s], 0, n_dst - 1)
            c = jnp.clip(cols_ref[s], 0, n_src - 1)
            tile = _masked_tile(tiles_ref, mask_ref, s, keep)
            acc_ref[r] += jnp.dot(tile, src_ref[c], preferred_element_type=jnp.float32)
        return carry

    lax.fori_loop(0, (n_live + UNROLL - 1) // UNROLL, body, 0)
    stage_ref[...] = acc_ref[...].astype(stage_ref.dtype)
    copy = pltpu.make_async_copy(stage_ref, out_ref.at[:, pl.ds(row_offset, BLOCK), :], sem)
    copy.start()
    copy.wait()


def _first_kernel(live_ref, rows_ref, cols_ref, tiles_ref, mask_ref, src_ref, shared_ref, out_ref, acc_ref, dacc_ref):
    slots = tiles_ref.shape[0]
    n_dst = acc_ref.shape[0]
    n_src = src_ref.shape[0]
    acc_ref[...] = jnp.zeros_like(acc_ref)
    dacc_ref[...] = jnp.zeros_like(dacc_ref)
    n_live = jnp.clip(live_ref[0], 0, slots)
    first_row = (lax.broadcasted_iota(jnp.int32, (8, BLOCK), 0) == 0).astype(jnp.bfloat16)

    def body(k, carry):
        for u in range(UNROLL):
            s, keep = _slot(k, u, n_live, slots)
            r = jnp.clip(rows_ref[s], 0, n_dst - 1)
            c = jnp.clip(cols_ref[s], 0, n_src - 1)
            tile = _masked_tile(tiles_ref, mask_ref, s, keep)
            acc_ref[r] += jnp.dot(tile, src_ref[c], preferred_element_type=jnp.float32)
            dacc_ref[r] += lax.dot_general(
                first_row, tile, (((1,), (1,)), ((), ())), preferred_element_type=jnp.float32
            )
        return carry

    lax.fori_loop(0, (n_live + UNROLL - 1) // UNROLL, body, 0)
    degree = jnp.sum(dacc_ref[...], axis=1).astype(out_ref.dtype)
    shared = shared_ref[...]
    n_deg = degree.shape[0]
    for t in range(n_dst):
        out_ref[t, 0:BLOCK, :] = acc_ref[t].astype(out_ref.dtype)
        out_ref[t, BLOCK : BLOCK + n_deg, :] = degree
        out_ref[t, BLOCK + n_deg :, :] = shared


def first_aggregate(live, rows, cols, tiles, mask, src, shared, n_dst):
    width = src.shape[-1]
    slots = tiles.shape[0]
    rows_out = BLOCK + n_dst + shared.shape[0]
    flops = 2 * slots * BLOCK * BLOCK * (width + 8)
    bytes_accessed = tiles.size * 2 + src.size * 2 + n_dst * rows_out * width * 2
    return pl.pallas_call(
        _first_kernel,
        out_shape=jax.ShapeDtypeStruct((n_dst, rows_out, width), jnp.bfloat16),
        in_specs=[_SMEM, _SMEM, _SMEM, _VMEM, _VMEM, _VMEM, _VMEM],
        out_specs=_VMEM,
        scratch_shapes=[
            pltpu.VMEM((n_dst, BLOCK, width), jnp.float32),
            pltpu.VMEM((n_dst, 8, BLOCK), jnp.float32),
        ],
        cost_estimate=pl.CostEstimate(flops=flops, bytes_accessed=bytes_accessed, transcendentals=0),
    )(live, rows, cols, tiles, mask, src, shared)


def _transpose_kernel(row_offset, live_ref, rows_ref, cols_ref, tiles_ref, mask_ref, src_ref, into_ref, out_ref,
                      acc_ref, stage_ref, sem):
    del into_ref
    slots = tiles_ref.shape[0]
    n_dst = acc_ref.shape[0]
    n_src = src_ref.shape[0]
    acc_ref[...] = jnp.zeros_like(acc_ref)
    n_live = jnp.clip(live_ref[0], 0, slots)

    def body(k, carry):
        for u in range(UNROLL):
            s, keep = _slot(k, u, n_live, slots)
            r = jnp.clip(rows_ref[s], 0, n_src - 1)
            c = jnp.clip(cols_ref[s], 0, n_dst - 1)
            tile = _masked_tile(tiles_ref, mask_ref, s, keep)
            acc_ref[c] += jnp.dot(src_ref[r], tile, preferred_element_type=jnp.float32)
        return carry

    lax.fori_loop(0, (n_live + UNROLL - 1) // UNROLL, body, 0)
    stage_ref[...] = acc_ref[...].astype(stage_ref.dtype)
    copy = pltpu.make_async_copy(stage_ref, out_ref.at[:, pl.ds(row_offset, BLOCK), :], sem)
    copy.start()
    copy.wait()


def _aggregate_into(kernel, live, rows, cols, tiles, mask, src, into, row_offset):
    n_dst = into.shape[0]
    width = into.shape[2]
    slots = tiles.shape[0]
    flops = 2 * slots * BLOCK * BLOCK * width
    bytes_accessed = tiles.size * 2 + src.size * 2 + n_dst * BLOCK * width * 2
    return pl.pallas_call(
        functools.partial(kernel, row_offset),
        out_shape=jax.ShapeDtypeStruct(into.shape, into.dtype),
        in_specs=[_SMEM, _SMEM, _SMEM, _VMEM, _VMEM, _VMEM, _ANY],
        out_specs=_ANY,
        scratch_shapes=[
            pltpu.VMEM((n_dst, BLOCK, width), jnp.float32),
            pltpu.VMEM((n_dst, BLOCK, width), into.dtype),
            pltpu.SemaphoreType.DMA(()),
        ],
        input_output_aliases={6: 0},
        cost_estimate=pl.CostEstimate(flops=flops, bytes_accessed=bytes_accessed, transcendentals=0),
    )(live, rows, cols, tiles, mask, src, into)


def forward_aggregate_into(live, rows, cols, tiles, mask, src, into, row_offset):
    return _aggregate_into(_forward_kernel, live, rows, cols, tiles, mask, src, into, row_offset)


def transpose_aggregate_into(live, rows, cols, tiles, mask, src_t, into, row_offset):
    return _aggregate_into(_transpose_kernel, live, rows, cols, tiles, mask, src_t, into, row_offset)


def gather_blocks(block, axis):
    n = lax.axis_size(axis)
    return lax.all_to_all(jnp.broadcast_to(block[None], (n,) + block.shape), axis, 0, 0, tiled=False)


def scatter_blocks(blocks, axis):
    return lax.all_to_all(blocks, axis, 0, 0, tiled=False)


def split_hi_lo(value):
    hi = value.astype(jnp.bfloat16)
    lo = (value - hi.astype(jnp.float32)).astype(jnp.bfloat16)
    return hi, lo


def local(
    features,
    first_weight,
    second_weight,
    tile_rows,
    tile_cols,
    tile_live,
    column_mask,
    edge_weight,
    cotangent,
):
    f32 = jnp.float32
    bf16 = jnp.bfloat16
    n_rows_axis = lax.axis_size("row")
    n_cols_axis = lax.axis_size("col")
    node_count = features.shape[0]
    row_groups = n_cols_axis * node_count // BLOCK
    col_groups = n_rows_axis * node_count // BLOCK

    live = tile_live.reshape(1)
    rows = tile_rows[0, 0]
    cols = tile_cols[0, 0]
    tiles = edge_weight[0, 0]
    mask = column_mask[0, 0]

    x_panel = gather_blocks(features, "row")
    packed = first_aggregate(live, rows, cols, tiles, mask, x_panel, cotangent.T, row_groups)
    arrived = scatter_blocks(packed, "col")
    summed_in = jnp.sum(arrived[:, :BLOCK].astype(f32), axis=0)
    degrees = jnp.sum(arrived[:, BLOCK : BLOCK + row_groups].astype(f32), axis=0)
    group_cot_t = arrived[:, BLOCK + row_groups :]
    group_scale = 1.0 / jnp.sqrt(1.0 + degrees)
    me = lax.axis_index("col")
    row_scale = lax.dynamic_index_in_dim(group_scale, me, axis=0, keepdims=False)[:, None]

    first_mix = (features.astype(f32) + row_scale * summed_in).astype(bf16)
    first_pre = jnp.dot(first_mix, first_weight, preferred_element_type=f32)
    hidden = gelu_tanh(first_pre).astype(bf16)
    projected = jnp.dot(hidden, second_weight, preferred_element_type=f32)

    grad_panel_t = (group_scale[:, None, :] * group_cot_t.astype(f32)).astype(bf16)
    packed = jnp.concatenate(
        [
            jnp.broadcast_to(projected.astype(bf16)[None], (col_groups, BLOCK, BLOCK)),
            jnp.zeros((col_groups, BLOCK, BLOCK), bf16),
        ],
        axis=1,
    )
    packed = transpose_aggregate_into(live, rows, cols, tiles, mask, grad_panel_t, packed, BLOCK)
    arrived = scatter_blocks(packed, "row")
    y_panel = arrived[:, :BLOCK]
    returned_t = jnp.sum(arrived[:, BLOCK:].astype(f32), axis=0)

    hp = lax.Precision.HIGHEST
    combined = cotangent.astype(f32) + returned_t.T
    hidden_grad = jnp.dot(combined, second_weight.astype(f32).T, precision=hp, preferred_element_type=f32)
    pre_grad = (hidden_grad * gelu_slope(first_pre)).astype(bf16)
    first_term = jnp.dot(first_mix.T, pre_grad, preferred_element_type=f32)
    second_term = jnp.dot(hidden.astype(f32).T, combined, precision=hp, preferred_element_type=f32)
    node_scale = 1.0 / math.sqrt(node_count * n_rows_axis * n_cols_axis)
    flat = jnp.concatenate([first_term.reshape(-1), second_term.reshape(-1)]) * node_scale
    slices = flat.reshape(row_groups, -1, BLOCK)

    packed = jnp.concatenate([jnp.zeros((row_groups, BLOCK, BLOCK), bf16), slices.astype(bf16)], axis=1)
    packed = forward_aggregate_into(live, rows, cols, tiles, mask, y_panel, packed, 0)
    arrived = scatter_blocks(packed, "col").astype(f32)
    summed_y = jnp.sum(arrived[:, :BLOCK], axis=0)
    output = (projected + row_scale * summed_y).astype(bf16)
    part = jnp.sum(arrived[:, BLOCK:], axis=0)

    total = jnp.sum(gather_blocks(part.astype(bf16), "row").astype(f32), axis=0)
    everything = gather_blocks(total.astype(bf16), "col").astype(f32).reshape(-1)
    split = first_term.size
    first_grad = everything[:split].reshape(first_term.shape)
    second_grad = everything[split:].reshape(second_term.shape)
    return (output, first_grad, second_grad)


def solution(mesh):
    return jax.shard_map(
        local,
        mesh=mesh,
        in_specs=(
            P(("row", "col"), None),
            P(),
            P(),
            P("row", "col", None),
            P("row", "col", None),
            P("row", "col"),
            P("row", "col", None, None),
            P("row", "col", None, None, None),
            P(("row", "col"), None),
        ),
        out_specs=(P(("row", "col"), None), P(), P()),
        check_vma=False,
    )
```

```python
import functools
import math

import jax
import jax.numpy as jnp
from jax import lax
from jax.experimental import pallas as pl
from jax.experimental.pallas import tpu as pltpu
from jax.sharding import PartitionSpec as P

BLOCK = 128


gelu_coef = math.sqrt(2.0 / math.pi)


def gelu_tanh(value):
    return 0.5 * value * (1.0 + jnp.tanh(gelu_coef * (value + 0.044715 * value * value * value)))


def gelu_slope(value):
    tanh_value = jnp.tanh(gelu_coef * (value + 0.044715 * value * value * value))
    return 0.5 * (1.0 + tanh_value) + 0.5 * value * (1.0 - tanh_value * tanh_value) * gelu_coef * (
        1.0 + 3.0 * 0.044715 * value * value
    )


UNROLL = 16


def _slot(k, u, n_live, slots):
    index = k * UNROLL + u
    return jnp.minimum(index, slots - 1), (index < n_live).astype(jnp.float32)


def _masked_tile(tiles_ref, mask_ref, s, keep):
    column = mask_ref[pl.ds(s, 1), :].astype(jnp.float32) * keep
    return (tiles_ref[s].astype(jnp.float32) * column).astype(jnp.bfloat16)


def _forward_kernel(row_offset, src_offset, live_ref, rows_ref, cols_ref, tiles_ref, mask_ref, src_ref, into_ref,
                    out_ref, acc_ref, stage_ref, sem):
    del into_ref
    slots = tiles_ref.shape[0]
    n_dst = acc_ref.shape[0]
    n_src = src_ref.shape[0]
    acc_ref[...] = jnp.zeros_like(acc_ref)
    n_live = jnp.clip(live_ref[0], 0, slots)

    def body(k, carry):
        for u in range(UNROLL):
            s, keep = _slot(k, u, n_live, slots)
            r = jnp.clip(rows_ref[s], 0, n_dst - 1)
            c = jnp.clip(cols_ref[s], 0, n_src - 1)
            tile = _masked_tile(tiles_ref, mask_ref, s, keep)
            source = src_ref[c, src_offset : src_offset + BLOCK, :]
            acc_ref[r] += jnp.dot(tile, source, preferred_element_type=jnp.float32)
        return carry

    lax.fori_loop(0, (n_live + UNROLL - 1) // UNROLL, body, 0)
    stage_ref[...] = acc_ref[...].astype(stage_ref.dtype)
    copy = pltpu.make_async_copy(stage_ref, out_ref.at[:, pl.ds(row_offset, BLOCK), :], sem)
    copy.start()
    copy.wait()


def _transpose_kernel(row_offset, src_offset, live_ref, rows_ref, cols_ref, tiles_ref, mask_ref, src_ref, scale_ref,
                      into_ref, out_ref, acc_ref, stage_ref, sem):
    del into_ref
    slots = tiles_ref.shape[0]
    n_dst = acc_ref.shape[0]
    n_src = src_ref.shape[0]
    acc_ref[...] = jnp.zeros_like(acc_ref)
    n_live = jnp.clip(live_ref[0], 0, slots)

    def body(k, carry):
        for u in range(UNROLL):
            s, keep = _slot(k, u, n_live, slots)
            r = jnp.clip(rows_ref[s], 0, n_src - 1)
            c = jnp.clip(cols_ref[s], 0, n_dst - 1)
            tile = _masked_tile(tiles_ref, mask_ref, s, keep)
            scale = scale_ref[pl.ds(r, 1), :]
            source = src_ref[r, src_offset : src_offset + BLOCK, :].astype(jnp.float32)
            source = (source * scale).astype(jnp.bfloat16)
            acc_ref[c] += jnp.dot(source, tile, preferred_element_type=jnp.float32)
        return carry

    lax.fori_loop(0, (n_live + UNROLL - 1) // UNROLL, body, 0)
    stage_ref[...] = acc_ref[...].astype(stage_ref.dtype)
    copy = pltpu.make_async_copy(stage_ref, out_ref.at[:, pl.ds(row_offset, BLOCK), :], sem)
    copy.start()
    copy.wait()


_SMEM = pl.BlockSpec(memory_space=pltpu.SMEM)
_VMEM = pl.BlockSpec(memory_space=pltpu.VMEM)
_ANY = pl.BlockSpec(memory_space=pl.ANY)


def _aggregate_into(kernel, operands, n_vmem, into, row_offset, src_offset, tiles, src_bytes):
    n_dst = into.shape[0]
    width = into.shape[2]
    slots = tiles.shape[0]
    flops = 2 * slots * BLOCK * BLOCK * width
    bytes_accessed = tiles.size * 2 + src_bytes + n_dst * BLOCK * width * 2
    return pl.pallas_call(
        functools.partial(kernel, row_offset, src_offset),
        out_shape=jax.ShapeDtypeStruct(into.shape, into.dtype),
        in_specs=[_SMEM, _SMEM, _SMEM] + [_VMEM] * n_vmem + [_ANY],
        out_specs=_ANY,
        scratch_shapes=[
            pltpu.VMEM((n_dst, BLOCK, width), jnp.float32),
            pltpu.VMEM((n_dst, BLOCK, width), into.dtype),
            pltpu.SemaphoreType.DMA(()),
        ],
        input_output_aliases={3 + n_vmem: 0},
        cost_estimate=pl.CostEstimate(flops=flops, bytes_accessed=bytes_accessed, transcendentals=0),
    )(*operands, into)


def forward_aggregate_into(live, rows, cols, tiles, mask, src, src_offset, into, row_offset):
    n_src = src.shape[0]
    return _aggregate_into(
        _forward_kernel, (live, rows, cols, tiles, mask, src), 3, into, row_offset, src_offset, tiles,
        n_src * BLOCK * BLOCK * 2,
    )


def transpose_aggregate_into(live, rows, cols, tiles, mask, src_t, src_offset, scale, into, row_offset):
    n_src = src_t.shape[0]
    return _aggregate_into(
        _transpose_kernel, (live, rows, cols, tiles, mask, src_t, scale), 4, into, row_offset, src_offset, tiles,
        n_src * BLOCK * BLOCK * 2,
    )


def gather_blocks(block, axis):
    n = lax.axis_size(axis)
    return lax.all_to_all(jnp.broadcast_to(block[None], (n,) + block.shape), axis, 0, 0, tiled=False)


def scatter_blocks(blocks, axis):
    return lax.all_to_all(blocks, axis, 0, 0, tiled=False)


def split_hi_lo(value):
    hi = value.astype(jnp.bfloat16)
    lo = (value - hi.astype(jnp.float32)).astype(jnp.bfloat16)
    return hi, lo


def local(
    features,
    first_weight,
    second_weight,
    tile_rows,
    tile_cols,
    tile_live,
    column_mask,
    edge_weight,
    cotangent,
):
    f32 = jnp.float32
    bf16 = jnp.bfloat16
    n_rows_axis = lax.axis_size("row")
    n_cols_axis = lax.axis_size("col")
    node_count = features.shape[0]
    row_groups = n_cols_axis * node_count // BLOCK
    col_groups = n_rows_axis * node_count // BLOCK

    live = tile_live.reshape(1)
    rows = tile_rows[0, 0]
    cols = tile_cols[0, 0]
    tiles = edge_weight[0, 0]
    mask = column_mask[0, 0]

    x_panel = gather_blocks(features, "row")
    live_weight = (jnp.arange(tiles.shape[0]) < jnp.clip(live[0], 0, tiles.shape[0])).astype(jnp.int32)
    live_mask = (mask * live_weight[:, None]).astype(bf16)
    row_sums = jnp.einsum("sij,sj->si", tiles, live_mask, preferred_element_type=f32)
    partial_deg = jnp.zeros((row_groups, BLOCK), f32).at[jnp.clip(rows, 0, row_groups - 1)].add(row_sums)
    shared = jnp.concatenate([partial_deg.astype(bf16), cotangent.T], axis=0)
    packed = jnp.concatenate(
        [jnp.zeros((row_groups, BLOCK, BLOCK), bf16), jnp.broadcast_to(shared[None], (row_groups,) + shared.shape)],
        axis=1,
    )
    packed = forward_aggregate_into(live, rows, cols, tiles, mask, x_panel, 0, packed, 0)
    arrived = scatter_blocks(packed, "col")
    summed_in = jnp.sum(arrived[:, :BLOCK].astype(f32), axis=0)
    degrees = jnp.sum(arrived[:, BLOCK : BLOCK + row_groups].astype(f32), axis=0)
    group_scale = 1.0 / jnp.sqrt(1.0 + degrees)
    me = lax.axis_index("col")
    row_scale = lax.dynamic_index_in_dim(group_scale, me, axis=0, keepdims=False)[:, None]

    first_mix = (features.astype(f32) + row_scale * summed_in).astype(bf16)
    first_pre = jnp.dot(first_mix, first_weight, preferred_element_type=f32)
    hidden = gelu_tanh(first_pre).astype(bf16)
    projected = jnp.dot(hidden, second_weight, preferred_element_type=f32)

    packed = jnp.concatenate(
        [
            jnp.broadcast_to(projected.astype(bf16)[None], (col_groups, BLOCK, BLOCK)),
            jnp.zeros((col_groups, BLOCK, BLOCK), bf16),
        ],
        axis=1,
    )
    packed = transpose_aggregate_into(
        live, rows, cols, tiles, mask, arrived, BLOCK + row_groups, group_scale, packed, BLOCK
    )
    arrived = scatter_blocks(packed, "row")
    returned_t = jnp.sum(arrived[:, BLOCK:].astype(f32), axis=0)

    hp = lax.Precision.HIGHEST
    combined = cotangent.astype(f32) + returned_t.T
    hidden_grad = jnp.dot(combined, second_weight.astype(f32).T, precision=hp, preferred_element_type=f32)
    pre_grad = (hidden_grad * gelu_slope(first_pre)).astype(bf16)
    first_term = jnp.dot(first_mix.T, pre_grad, preferred_element_type=f32)
    second_term = jnp.dot(hidden.astype(f32).T, combined, precision=hp, preferred_element_type=f32)
    node_scale = 1.0 / math.sqrt(node_count * n_rows_axis * n_cols_axis)
    flat = jnp.concatenate([first_term.reshape(-1), second_term.reshape(-1)]) * node_scale
    slices = flat.reshape(row_groups, -1, BLOCK)

    packed = jnp.concatenate([jnp.zeros((row_groups, BLOCK, BLOCK), bf16), slices.astype(bf16)], axis=1)
    packed = forward_aggregate_into(live, rows, cols, tiles, mask, arrived, 0, packed, 0)
    arrived = scatter_blocks(packed, "col").astype(f32)
    summed_y = jnp.sum(arrived[:, :BLOCK], axis=0)
    output = (projected + row_scale * summed_y).astype(bf16)
    part = jnp.sum(arrived[:, BLOCK:], axis=0)

    total = jnp.sum(gather_blocks(part.astype(bf16), "row").astype(f32), axis=0)
    everything = gather_blocks(total.astype(bf16), "col").astype(f32).reshape(-1)
    split = first_term.size
    first_grad = everything[:split].reshape(first_term.shape)
    second_grad = everything[split:].reshape(second_term.shape)
    return (output, first_grad, second_grad)


def solution(mesh):
    return jax.shard_map(
        local,
        mesh=mesh,
        in_specs=(
            P(("row", "col"), None),
            P(),
            P(),
            P("row", "col", None),
            P("row", "col", None),
            P("row", "col"),
            P("row", "col", None, None),
            P("row", "col", None, None, None),
            P(("row", "col"), None),
        ),
        out_specs=(P(("row", "col"), None), P(), P()),
        check_vma=False,
    )
```

```python
import functools
import math

import jax
import jax.numpy as jnp
from jax import lax
from jax.experimental import pallas as pl
from jax.experimental.pallas import tpu as pltpu
from jax.sharding import PartitionSpec as P

BLOCK = 128


gelu_coef = math.sqrt(2.0 / math.pi)


def gelu_tanh(value):
    return 0.5 * value * (1.0 + jnp.tanh(gelu_coef * (value + 0.044715 * value * value * value)))


def gelu_slope(value):
    tanh_value = jnp.tanh(gelu_coef * (value + 0.044715 * value * value * value))
    return 0.5 * (1.0 + tanh_value) + 0.5 * value * (1.0 - tanh_value * tanh_value) * gelu_coef * (
        1.0 + 3.0 * 0.044715 * value * value
    )


UNROLL = 16


def _slot(k, u, n_live, slots):
    index = k * UNROLL + u
    return jnp.minimum(index, slots - 1), (index < n_live).astype(jnp.float32)


def _masked_tile(tiles_ref, mask_ref, s, keep):
    column = mask_ref[pl.ds(s, 1), :].astype(jnp.float32) * keep
    return (tiles_ref[s].astype(jnp.float32) * column).astype(jnp.bfloat16)


def _forward_kernel(row_offset, src_offset, live_ref, rows_ref, cols_ref, tiles_ref, mask_ref, src_ref, into_ref,
                    out_ref, acc_ref, stage_ref, sem):
    del into_ref
    slots = tiles_ref.shape[0]
    n_dst = acc_ref.shape[0]
    n_src = src_ref.shape[0]
    acc_ref[...] = jnp.zeros_like(acc_ref)
    n_live = jnp.clip(live_ref[0], 0, slots)

    def body(k, carry):
        for u in range(UNROLL):
            s, keep = _slot(k, u, n_live, slots)
            r = jnp.clip(rows_ref[s], 0, n_dst - 1)
            c = jnp.clip(cols_ref[s], 0, n_src - 1)
            tile = _masked_tile(tiles_ref, mask_ref, s, keep)
            source = src_ref[c, src_offset : src_offset + BLOCK, :]
            acc_ref[r] += jnp.dot(tile, source, preferred_element_type=jnp.float32)
        return carry

    lax.fori_loop(0, (n_live + UNROLL - 1) // UNROLL, body, 0)
    stage_ref[...] = acc_ref[...].astype(stage_ref.dtype)
    copy = pltpu.make_async_copy(stage_ref, out_ref.at[:, pl.ds(row_offset, BLOCK), :], sem)
    copy.start()
    copy.wait()


def _transpose_kernel(row_offset, src_offset, live_ref, rows_ref, cols_ref, tiles_ref, mask_ref, src_ref, scale_ref,
                      into_ref, out_ref, acc_ref, stage_ref, sem):
    del into_ref
    slots = tiles_ref.shape[0]
    n_dst = acc_ref.shape[0]
    n_src = src_ref.shape[0]
    acc_ref[...] = jnp.zeros_like(acc_ref)
    n_live = jnp.clip(live_ref[0], 0, slots)

    def body(k, carry):
        for u in range(UNROLL):
            s, keep = _slot(k, u, n_live, slots)
            r = jnp.clip(rows_ref[s], 0, n_src - 1)
            c = jnp.clip(cols_ref[s], 0, n_dst - 1)
            tile = _masked_tile(tiles_ref, mask_ref, s, keep)
            scale = scale_ref[pl.ds(r, 1), :]
            source = src_ref[r, src_offset : src_offset + BLOCK, :].astype(jnp.float32)
            source = (source * scale).astype(jnp.bfloat16)
            acc_ref[c] += jnp.dot(source, tile, preferred_element_type=jnp.float32)
        return carry

    lax.fori_loop(0, (n_live + UNROLL - 1) // UNROLL, body, 0)
    stage_ref[...] = acc_ref[...].astype(stage_ref.dtype)
    copy = pltpu.make_async_copy(stage_ref, out_ref.at[:, pl.ds(row_offset, BLOCK), :], sem)
    copy.start()
    copy.wait()


_SMEM = pl.BlockSpec(memory_space=pltpu.SMEM)
_VMEM = pl.BlockSpec(memory_space=pltpu.VMEM)
_ANY = pl.BlockSpec(memory_space=pl.ANY)


def _aggregate_into(kernel, operands, n_vmem, into, row_offset, src_offset, tiles, src_bytes):
    n_dst = into.shape[0]
    width = into.shape[2]
    slots = tiles.shape[0]
    flops = 2 * slots * BLOCK * BLOCK * width
    bytes_accessed = tiles.size * 2 + src_bytes + n_dst * BLOCK * width * 2
    return pl.pallas_call(
        functools.partial(kernel, row_offset, src_offset),
        out_shape=jax.ShapeDtypeStruct(into.shape, into.dtype),
        in_specs=[_SMEM, _SMEM, _SMEM] + [_VMEM] * n_vmem + [_ANY],
        out_specs=_ANY,
        scratch_shapes=[
            pltpu.VMEM((n_dst, BLOCK, width), jnp.float32),
            pltpu.VMEM((n_dst, BLOCK, width), into.dtype),
            pltpu.SemaphoreType.DMA(()),
        ],
        input_output_aliases={3 + n_vmem: 0},
        cost_estimate=pl.CostEstimate(flops=flops, bytes_accessed=bytes_accessed, transcendentals=0),
    )(*operands, into)


def forward_aggregate_into(live, rows, cols, tiles, mask, src, src_offset, into, row_offset):
    n_src = src.shape[0]
    return _aggregate_into(
        _forward_kernel, (live, rows, cols, tiles, mask, src), 3, into, row_offset, src_offset, tiles,
        n_src * BLOCK * BLOCK * 2,
    )


def transpose_aggregate_into(live, rows, cols, tiles, mask, src_t, src_offset, scale, into, row_offset):
    n_src = src_t.shape[0]
    return _aggregate_into(
        _transpose_kernel, (live, rows, cols, tiles, mask, src_t, scale), 4, into, row_offset, src_offset, tiles,
        n_src * BLOCK * BLOCK * 2,
    )


def gather_blocks(block, axis):
    n = lax.axis_size(axis)
    return lax.all_to_all(jnp.broadcast_to(block[None], (n,) + block.shape), axis, 0, 0, tiled=False)


def scatter_blocks(blocks, axis):
    return lax.all_to_all(blocks, axis, 0, 0, tiled=False)


def split_hi_lo(value):
    hi = value.astype(jnp.bfloat16)
    lo = (value - hi.astype(jnp.float32)).astype(jnp.bfloat16)
    return hi, lo


def local(
    features,
    first_weight,
    second_weight,
    tile_rows,
    tile_cols,
    tile_live,
    column_mask,
    edge_weight,
    cotangent,
):
    f32 = jnp.float32
    bf16 = jnp.bfloat16
    n_rows_axis = lax.axis_size("row")
    n_cols_axis = lax.axis_size("col")
    node_count = features.shape[0]
    row_groups = n_cols_axis * node_count // BLOCK
    col_groups = n_rows_axis * node_count // BLOCK

    live = tile_live.reshape(1)
    rows = tile_rows[0, 0]
    cols = tile_cols[0, 0]
    tiles = edge_weight[0, 0]
    mask = column_mask[0, 0]

    x_panel = gather_blocks(features, "row")
    live_weight = (jnp.arange(tiles.shape[0]) < jnp.clip(live[0], 0, tiles.shape[0])).astype(jnp.int32)
    live_mask = (mask * live_weight[:, None]).astype(bf16)
    row_sums = jnp.einsum("sij,sj->si", tiles, live_mask, preferred_element_type=f32)
    partial_deg = jnp.zeros((row_groups, BLOCK), f32).at[jnp.clip(rows, 0, row_groups - 1)].add(row_sums)
    shared = jnp.concatenate([partial_deg.astype(bf16), cotangent.T], axis=0)
    packed = jnp.concatenate(
        [jnp.zeros((row_groups, BLOCK, BLOCK), bf16), jnp.broadcast_to(shared[None], (row_groups,) + shared.shape)],
        axis=1,
    )
    packed = forward_aggregate_into(live, rows, cols, tiles, mask, x_panel, 0, packed, 0)
    arrived = scatter_blocks(packed, "col")
    summed_in = jnp.sum(arrived[:, :BLOCK].astype(f32), axis=0)
    degrees = jnp.sum(arrived[:, BLOCK : BLOCK + row_groups].astype(f32), axis=0)
    group_scale = 1.0 / jnp.sqrt(1.0 + degrees)
    me = lax.axis_index("col")
    row_scale = lax.dynamic_index_in_dim(group_scale, me, axis=0, keepdims=False)[:, None]

    first_mix = (features.astype(f32) + row_scale * summed_in).astype(bf16)
    first_pre = jnp.dot(first_mix, first_weight, preferred_element_type=f32)
    hidden = gelu_tanh(first_pre).astype(bf16)
    projected = jnp.dot(hidden, second_weight, preferred_element_type=f32)

    packed = jnp.concatenate(
        [
            jnp.broadcast_to(projected.astype(bf16)[None], (col_groups, BLOCK, BLOCK)),
            jnp.zeros((col_groups, BLOCK, BLOCK), bf16),
        ],
        axis=1,
    )
    packed = transpose_aggregate_into(
        live, rows, cols, tiles, mask, arrived, BLOCK + row_groups, group_scale, packed, BLOCK
    )
    arrived = scatter_blocks(packed, "row")
    returned_t = jnp.sum(arrived[:, BLOCK:].astype(f32), axis=0)

    hp = lax.Precision.HIGHEST
    combined = cotangent.astype(f32) + returned_t.T
    hidden_grad = jnp.dot(combined, second_weight.astype(f32).T, precision=hp, preferred_element_type=f32)
    pre_grad = (hidden_grad * gelu_slope(first_pre)).astype(bf16)
    first_term_t = lax.dot_general(pre_grad, first_mix, (((0,), (0,)), ((), ())), preferred_element_type=f32)
    second_term = jnp.dot(hidden.astype(f32).T, combined, precision=hp, preferred_element_type=f32)
    node_scale = 1.0 / math.sqrt(node_count * n_rows_axis * n_cols_axis)
    flat = jnp.concatenate([first_term_t, second_term], axis=0) * node_scale
    slices = flat.reshape(row_groups, -1, BLOCK)

    packed = jnp.concatenate([jnp.zeros((row_groups, BLOCK, BLOCK), bf16), slices.astype(bf16)], axis=1)
    packed = forward_aggregate_into(live, rows, cols, tiles, mask, arrived, 0, packed, 0)
    arrived = scatter_blocks(packed, "col").astype(f32)
    summed_y = jnp.sum(arrived[:, :BLOCK], axis=0)
    output = (projected + row_scale * summed_y).astype(bf16)
    part = jnp.sum(arrived[:, BLOCK:], axis=0)

    total = jnp.sum(gather_blocks(part.astype(bf16), "row").astype(f32), axis=0)
    everything = gather_blocks(total.astype(bf16), "col").astype(f32).reshape(-1, BLOCK)
    split = first_term_t.shape[0]
    first_grad = everything[:split].T
    second_grad = everything[split:]
    return (output, first_grad, second_grad)


def solution(mesh):
    return jax.shard_map(
        local,
        mesh=mesh,
        in_specs=(
            P(("row", "col"), None),
            P(),
            P(),
            P("row", "col", None),
            P("row", "col", None),
            P("row", "col"),
            P("row", "col", None, None),
            P("row", "col", None, None, None),
            P(("row", "col"), None),
        ),
        out_specs=(P(("row", "col"), None), P(), P()),
        check_vma=False,
    )
```

```python
import functools
import math

import jax
import jax.numpy as jnp
from jax import lax
from jax.experimental import pallas as pl
from jax.experimental.pallas import tpu as pltpu
from jax.sharding import PartitionSpec as P

BLOCK = 128


gelu_coef = math.sqrt(2.0 / math.pi)


def gelu_tanh(value):
    return 0.5 * value * (1.0 + jnp.tanh(gelu_coef * (value + 0.044715 * value * value * value)))


def gelu_slope(value):
    tanh_value = jnp.tanh(gelu_coef * (value + 0.044715 * value * value * value))
    return 0.5 * (1.0 + tanh_value) + 0.5 * value * (1.0 - tanh_value * tanh_value) * gelu_coef * (
        1.0 + 3.0 * 0.044715 * value * value
    )


UNROLL = 16


def _slot(k, u, n_live, slots):
    index = k * UNROLL + u
    return jnp.minimum(index, slots - 1), (index < n_live).astype(jnp.float32)


def _masked_tile(tiles_ref, mask_ref, s, keep):
    column = mask_ref[pl.ds(s, 1), :].astype(jnp.float32) * keep
    return (tiles_ref[s].astype(jnp.float32) * column).astype(jnp.bfloat16)


def _forward_kernel(row_offset, src_offset, live_ref, rows_ref, cols_ref, tiles_ref, mask_ref, src_ref, into_ref,
                    out_ref, acc_ref, stage_ref, sem):
    del into_ref
    slots = tiles_ref.shape[0]
    n_dst = acc_ref.shape[0]
    n_src = src_ref.shape[0]
    acc_ref[...] = jnp.zeros_like(acc_ref)
    n_live = jnp.clip(live_ref[0], 0, slots)

    def body(k, carry):
        for u in range(UNROLL):
            s, keep = _slot(k, u, n_live, slots)
            r = jnp.clip(rows_ref[s], 0, n_dst - 1)
            c = jnp.clip(cols_ref[s], 0, n_src - 1)
            tile = _masked_tile(tiles_ref, mask_ref, s, keep)
            source = src_ref[c, src_offset : src_offset + BLOCK, :]
            acc_ref[r] += jnp.dot(tile, source, preferred_element_type=jnp.float32)
        return carry

    lax.fori_loop(0, (n_live + UNROLL - 1) // UNROLL, body, 0)
    stage_ref[...] = acc_ref[...].astype(stage_ref.dtype)
    copy = pltpu.make_async_copy(stage_ref, out_ref.at[:, pl.ds(row_offset, BLOCK), :], sem)
    copy.start()
    copy.wait()


def _transpose_kernel(row_offset, src_offset, live_ref, rows_ref, cols_ref, tiles_ref, mask_ref, src_ref, scale_ref,
                      into_ref, out_ref, acc_ref, stage_ref, sem):
    del into_ref
    slots = tiles_ref.shape[0]
    n_dst = acc_ref.shape[0]
    n_src = src_ref.shape[0]
    acc_ref[...] = jnp.zeros_like(acc_ref)
    n_live = jnp.clip(live_ref[0], 0, slots)

    def body(k, carry):
        for u in range(UNROLL):
            s, keep = _slot(k, u, n_live, slots)
            r = jnp.clip(rows_ref[s], 0, n_src - 1)
            c = jnp.clip(cols_ref[s], 0, n_dst - 1)
            tile = _masked_tile(tiles_ref, mask_ref, s, keep)
            scale = scale_ref[pl.ds(r, 1), :]
            source = src_ref[r, src_offset : src_offset + BLOCK, :].astype(jnp.float32)
            source = (source * scale).astype(jnp.bfloat16)
            acc_ref[c] += jnp.dot(source, tile, preferred_element_type=jnp.float32)
        return carry

    lax.fori_loop(0, (n_live + UNROLL - 1) // UNROLL, body, 0)
    stage_ref[...] = acc_ref[...].astype(stage_ref.dtype)
    copy = pltpu.make_async_copy(stage_ref, out_ref.at[:, pl.ds(row_offset, BLOCK), :], sem)
    copy.start()
    copy.wait()


_SMEM = pl.BlockSpec(memory_space=pltpu.SMEM)
_VMEM = pl.BlockSpec(memory_space=pltpu.VMEM)
_ANY = pl.BlockSpec(memory_space=pl.ANY)


def _aggregate_into(kernel, operands, n_vmem, into, row_offset, src_offset, tiles, src_bytes):
    n_dst = into.shape[0]
    width = into.shape[2]
    slots = tiles.shape[0]
    flops = 2 * slots * BLOCK * BLOCK * width
    bytes_accessed = tiles.size * 2 + src_bytes + n_dst * BLOCK * width * 2
    return pl.pallas_call(
        functools.partial(kernel, row_offset, src_offset),
        out_shape=jax.ShapeDtypeStruct(into.shape, into.dtype),
        in_specs=[_SMEM, _SMEM, _SMEM] + [_VMEM] * n_vmem + [_ANY],
        out_specs=_ANY,
        scratch_shapes=[
            pltpu.VMEM((n_dst, BLOCK, width), jnp.float32),
            pltpu.VMEM((n_dst, BLOCK, width), into.dtype),
            pltpu.SemaphoreType.DMA(()),
        ],
        input_output_aliases={3 + n_vmem: 0},
        cost_estimate=pl.CostEstimate(flops=flops, bytes_accessed=bytes_accessed, transcendentals=0),
    )(*operands, into)


def forward_aggregate_into(live, rows, cols, tiles, mask, src, src_offset, into, row_offset):
    n_src = src.shape[0]
    return _aggregate_into(
        _forward_kernel, (live, rows, cols, tiles, mask, src), 3, into, row_offset, src_offset, tiles,
        n_src * BLOCK * BLOCK * 2,
    )


def transpose_aggregate_into(live, rows, cols, tiles, mask, src_t, src_offset, scale, into, row_offset):
    n_src = src_t.shape[0]
    return _aggregate_into(
        _transpose_kernel, (live, rows, cols, tiles, mask, src_t, scale), 4, into, row_offset, src_offset, tiles,
        n_src * BLOCK * BLOCK * 2,
    )


def gather_blocks(block, axis):
    n = lax.axis_size(axis)
    return lax.all_to_all(jnp.broadcast_to(block[None], (n,) + block.shape), axis, 0, 0, tiled=False)


def scatter_blocks(blocks, axis):
    return lax.all_to_all(blocks, axis, 0, 0, tiled=False)


def split_hi_lo(value):
    hi = value.astype(jnp.bfloat16)
    lo = (value - hi.astype(jnp.float32)).astype(jnp.bfloat16)
    return hi, lo


def local(
    features,
    first_weight,
    second_weight,
    tile_rows,
    tile_cols,
    tile_live,
    column_mask,
    edge_weight,
    cotangent,
):
    f32 = jnp.float32
    bf16 = jnp.bfloat16
    n_rows_axis = lax.axis_size("row")
    n_cols_axis = lax.axis_size("col")
    node_count = features.shape[0]
    row_groups = n_cols_axis * node_count // BLOCK
    col_groups = n_rows_axis * node_count // BLOCK

    live = tile_live.reshape(1)
    rows = tile_rows[0, 0]
    cols = tile_cols[0, 0]
    tiles = edge_weight[0, 0]
    mask = column_mask[0, 0]

    x_panel = gather_blocks(features, "row")
    live_weight = (jnp.arange(tiles.shape[0]) < jnp.clip(live[0], 0, tiles.shape[0])).astype(jnp.int32)
    live_mask = (mask * live_weight[:, None]).astype(bf16)
    row_sums = jnp.einsum("sij,sj->si", tiles, live_mask, preferred_element_type=f32)
    partial_deg = jnp.zeros((row_groups, BLOCK), f32).at[jnp.clip(rows, 0, row_groups - 1)].add(row_sums)
    shared = jnp.concatenate([partial_deg.astype(bf16), cotangent.T], axis=0)
    arrived_shared = gather_blocks(shared, "col")
    packed = jnp.zeros((row_groups, BLOCK, BLOCK), bf16)
    packed = forward_aggregate_into(live, rows, cols, tiles, mask, x_panel, 0, packed, 0)
    arrived = scatter_blocks(packed, "col")
    summed_in = jnp.sum(arrived.astype(f32), axis=0)
    degrees = jnp.sum(arrived_shared[:, :row_groups].astype(f32), axis=0)
    group_scale = 1.0 / jnp.sqrt(1.0 + degrees)
    me = lax.axis_index("col")
    row_scale = lax.dynamic_index_in_dim(group_scale, me, axis=0, keepdims=False)[:, None]

    first_mix = (features.astype(f32) + row_scale * summed_in).astype(bf16)
    first_pre = jnp.dot(first_mix, first_weight, preferred_element_type=f32)
    hidden = gelu_tanh(first_pre).astype(bf16)
    projected = jnp.dot(hidden, second_weight, preferred_element_type=f32)

    packed = jnp.concatenate(
        [
            jnp.broadcast_to(projected.astype(bf16)[None], (col_groups, BLOCK, BLOCK)),
            jnp.zeros((col_groups, BLOCK, BLOCK), bf16),
        ],
        axis=1,
    )
    packed = transpose_aggregate_into(
        live, rows, cols, tiles, mask, arrived_shared, row_groups, group_scale, packed, BLOCK
    )
    arrived = scatter_blocks(packed, "row")
    returned_t = jnp.sum(arrived[:, BLOCK:].astype(f32), axis=0)

    hp = lax.Precision.HIGHEST
    combined = cotangent.astype(f32) + returned_t.T
    hidden_grad = jnp.dot(combined, second_weight.astype(f32).T, precision=hp, preferred_element_type=f32)
    pre_grad = (hidden_grad * gelu_slope(first_pre)).astype(bf16)
    first_term = jnp.dot(first_mix.T, pre_grad, preferred_element_type=f32)
    second_term = jnp.dot(hidden.astype(f32).T, combined, precision=hp, preferred_element_type=f32)
    node_scale = 1.0 / math.sqrt(node_count * n_rows_axis * n_cols_axis)
    flat = jnp.concatenate([first_term.reshape(-1), second_term.reshape(-1)]) * node_scale
    slices = flat.reshape(row_groups, -1, BLOCK)

    packed = jnp.concatenate([jnp.zeros((row_groups, BLOCK, BLOCK), bf16), slices.astype(bf16)], axis=1)
    packed = forward_aggregate_into(live, rows, cols, tiles, mask, arrived, 0, packed, 0)
    arrived = scatter_blocks(packed, "col").astype(f32)
    summed_y = jnp.sum(arrived[:, :BLOCK], axis=0)
    output = (projected + row_scale * summed_y).astype(bf16)
    part = jnp.sum(arrived[:, BLOCK:], axis=0)

    total = jnp.sum(gather_blocks(part.astype(bf16), "row").astype(f32), axis=0)
    everything = gather_blocks(total.astype(bf16), "col").astype(f32).reshape(-1)
    split = first_term.size
    first_grad = everything[:split].reshape(first_term.shape)
    second_grad = everything[split:].reshape(second_term.shape)
    return (output, first_grad, second_grad)


def solution(mesh):
    return jax.shard_map(
        local,
        mesh=mesh,
        in_specs=(
            P(("row", "col"), None),
            P(),
            P(),
            P("row", "col", None),
            P("row", "col", None),
            P("row", "col"),
            P("row", "col", None, None),
            P("row", "col", None, None, None),
            P(("row", "col"), None),
        ),
        out_specs=(P(("row", "col"), None), P(), P()),
        check_vma=False,
    )
```

```python
import functools
import math

import jax
import jax.numpy as jnp
from jax import lax
from jax.experimental import pallas as pl
from jax.experimental.pallas import tpu as pltpu
from jax.sharding import PartitionSpec as P

BLOCK = 128


gelu_coef = math.sqrt(2.0 / math.pi)


def gelu_tanh(value):
    return 0.5 * value * (1.0 + jnp.tanh(gelu_coef * (value + 0.044715 * value * value * value)))


def gelu_slope(value):
    tanh_value = jnp.tanh(gelu_coef * (value + 0.044715 * value * value * value))
    return 0.5 * (1.0 + tanh_value) + 0.5 * value * (1.0 - tanh_value * tanh_value) * gelu_coef * (
        1.0 + 3.0 * 0.044715 * value * value
    )


UNROLL = 16


def _slot(k, u, n_live, slots):
    index = k * UNROLL + u
    return jnp.minimum(index, slots - 1), (index < n_live).astype(jnp.float32)


def _masked_tile(tiles_ref, mask_ref, s, keep):
    column = mask_ref[pl.ds(s, 1), :].astype(jnp.float32) * keep
    return (tiles_ref[s].astype(jnp.float32) * column).astype(jnp.bfloat16)


def _forward_kernel(row_offset, src_offset, extra_offset, live_ref, rows_ref, cols_ref, tiles_ref, mask_ref, src_ref,
                    extra_ref, into_ref, out_ref, acc_ref, stage_ref, sem, extra_sem):
    del into_ref
    extra_copy = pltpu.make_async_copy(
        extra_ref, out_ref.at[:, pl.ds(extra_offset, extra_ref.shape[1]), :], extra_sem
    )
    extra_copy.start()
    slots = tiles_ref.shape[0]
    n_dst = acc_ref.shape[0]
    n_src = src_ref.shape[0]
    acc_ref[...] = jnp.zeros_like(acc_ref)
    n_live = jnp.clip(live_ref[0], 0, slots)

    def body(k, carry):
        for u in range(UNROLL):
            s, keep = _slot(k, u, n_live, slots)
            r = jnp.clip(rows_ref[s], 0, n_dst - 1)
            c = jnp.clip(cols_ref[s], 0, n_src - 1)
            tile = _masked_tile(tiles_ref, mask_ref, s, keep)
            source = src_ref[c, src_offset : src_offset + BLOCK, :]
            acc_ref[r] += jnp.dot(tile, source, preferred_element_type=jnp.float32)
        return carry

    lax.fori_loop(0, (n_live + UNROLL - 1) // UNROLL, body, 0)
    stage_ref[...] = acc_ref[...].astype(stage_ref.dtype)
    copy = pltpu.make_async_copy(stage_ref, out_ref.at[:, pl.ds(row_offset, BLOCK), :], sem)
    copy.start()
    copy.wait()
    extra_copy.wait()


def _transpose_kernel(row_offset, src_offset, extra_offset, live_ref, rows_ref, cols_ref, tiles_ref, mask_ref,
                      src_ref, scale_ref, extra_ref, into_ref, out_ref, acc_ref, stage_ref, sem, extra_sem):
    del into_ref
    extra_copy = pltpu.make_async_copy(
        extra_ref, out_ref.at[:, pl.ds(extra_offset, extra_ref.shape[1]), :], extra_sem
    )
    extra_copy.start()
    slots = tiles_ref.shape[0]
    n_dst = acc_ref.shape[0]
    n_src = src_ref.shape[0]
    acc_ref[...] = jnp.zeros_like(acc_ref)
    n_live = jnp.clip(live_ref[0], 0, slots)

    def body(k, carry):
        for u in range(UNROLL):
            s, keep = _slot(k, u, n_live, slots)
            r = jnp.clip(rows_ref[s], 0, n_src - 1)
            c = jnp.clip(cols_ref[s], 0, n_dst - 1)
            tile = _masked_tile(tiles_ref, mask_ref, s, keep)
            scale = scale_ref[pl.ds(r, 1), :]
            source = src_ref[r, src_offset : src_offset + BLOCK, :].astype(jnp.float32)
            source = (source * scale).astype(jnp.bfloat16)
            acc_ref[c] += jnp.dot(source, tile, preferred_element_type=jnp.float32)
        return carry

    lax.fori_loop(0, (n_live + UNROLL - 1) // UNROLL, body, 0)
    stage_ref[...] = acc_ref[...].astype(stage_ref.dtype)
    copy = pltpu.make_async_copy(stage_ref, out_ref.at[:, pl.ds(row_offset, BLOCK), :], sem)
    copy.start()
    copy.wait()
    extra_copy.wait()


_SMEM = pl.BlockSpec(memory_space=pltpu.SMEM)
_VMEM = pl.BlockSpec(memory_space=pltpu.VMEM)
_ANY = pl.BlockSpec(memory_space=pl.ANY)


def _aggregate_into(kernel, operands, n_vmem, into, row_offset, src_offset, extra_offset, tiles, src_bytes):
    n_dst = into.shape[0]
    width = into.shape[2]
    slots = tiles.shape[0]
    flops = 2 * slots * BLOCK * BLOCK * width
    bytes_accessed = tiles.size * 2 + src_bytes + n_dst * BLOCK * width * 2
    return pl.pallas_call(
        functools.partial(kernel, row_offset, src_offset, extra_offset),
        out_shape=jax.ShapeDtypeStruct(into.shape, into.dtype),
        in_specs=[_SMEM, _SMEM, _SMEM] + [_VMEM] * n_vmem + [_ANY],
        out_specs=_ANY,
        scratch_shapes=[
            pltpu.VMEM((n_dst, BLOCK, width), jnp.float32),
            pltpu.VMEM((n_dst, BLOCK, width), into.dtype),
            pltpu.SemaphoreType.DMA(()),
            pltpu.SemaphoreType.DMA(()),
        ],
        input_output_aliases={3 + n_vmem: 0},
        cost_estimate=pl.CostEstimate(flops=flops, bytes_accessed=bytes_accessed, transcendentals=0),
    )(*operands, into)


def forward_aggregate_into(live, rows, cols, tiles, mask, src, src_offset, extra, extra_offset, into, row_offset):
    n_src = src.shape[0]
    return _aggregate_into(
        _forward_kernel, (live, rows, cols, tiles, mask, src, extra), 4, into, row_offset, src_offset,
        extra_offset, tiles, n_src * BLOCK * BLOCK * 2,
    )


def transpose_aggregate_into(live, rows, cols, tiles, mask, src_t, src_offset, scale, extra, extra_offset, into,
                             row_offset):
    n_src = src_t.shape[0]
    return _aggregate_into(
        _transpose_kernel, (live, rows, cols, tiles, mask, src_t, scale, extra), 5, into, row_offset, src_offset,
        extra_offset, tiles, n_src * BLOCK * BLOCK * 2,
    )


def gather_blocks(block, axis):
    n = lax.axis_size(axis)
    return lax.all_to_all(jnp.broadcast_to(block[None], (n,) + block.shape), axis, 0, 0, tiled=False)


def scatter_blocks(blocks, axis):
    return lax.all_to_all(blocks, axis, 0, 0, tiled=False)


def split_hi_lo(value):
    hi = value.astype(jnp.bfloat16)
    lo = (value - hi.astype(jnp.float32)).astype(jnp.bfloat16)
    return hi, lo


def local(
    features,
    first_weight,
    second_weight,
    tile_rows,
    tile_cols,
    tile_live,
    column_mask,
    edge_weight,
    cotangent,
):
    f32 = jnp.float32
    bf16 = jnp.bfloat16
    n_rows_axis = lax.axis_size("row")
    n_cols_axis = lax.axis_size("col")
    node_count = features.shape[0]
    row_groups = n_cols_axis * node_count // BLOCK
    col_groups = n_rows_axis * node_count // BLOCK

    live = tile_live.reshape(1)
    rows = tile_rows[0, 0]
    cols = tile_cols[0, 0]
    tiles = edge_weight[0, 0]
    mask = column_mask[0, 0]

    x_panel = gather_blocks(features, "row")
    live_weight = (jnp.arange(tiles.shape[0]) < jnp.clip(live[0], 0, tiles.shape[0])).astype(jnp.int32)
    live_mask = (mask * live_weight[:, None]).astype(bf16)
    row_sums = jnp.einsum("sij,sj->si", tiles, live_mask, preferred_element_type=f32)
    partial_deg = jnp.zeros((row_groups, BLOCK), f32).at[jnp.clip(rows, 0, row_groups - 1)].add(row_sums)
    shared = jnp.concatenate([partial_deg.astype(bf16), cotangent.T], axis=0)
    packed = jnp.zeros((row_groups, BLOCK + shared.shape[0], BLOCK), bf16)
    packed = forward_aggregate_into(
        live, rows, cols, tiles, mask, x_panel, 0,
        jnp.broadcast_to(shared[None], (row_groups,) + shared.shape), BLOCK, packed, 0,
    )
    arrived = scatter_blocks(packed, "col")
    summed_in = jnp.sum(arrived[:, :BLOCK].astype(f32), axis=0)
    degrees = jnp.sum(arrived[:, BLOCK : BLOCK + row_groups].astype(f32), axis=0)
    group_scale = 1.0 / jnp.sqrt(1.0 + degrees)
    me = lax.axis_index("col")
    row_scale = lax.dynamic_index_in_dim(group_scale, me, axis=0, keepdims=False)[:, None]

    first_mix = (features.astype(f32) + row_scale * summed_in).astype(bf16)
    first_pre = jnp.dot(first_mix, first_weight, preferred_element_type=f32)
    hidden = gelu_tanh(first_pre).astype(bf16)
    projected = jnp.dot(hidden, second_weight, preferred_element_type=f32)

    packed = jnp.zeros((col_groups, 2 * BLOCK, BLOCK), bf16)
    packed = transpose_aggregate_into(
        live, rows, cols, tiles, mask, arrived, BLOCK + row_groups, group_scale,
        jnp.broadcast_to(projected.astype(bf16)[None], (col_groups, BLOCK, BLOCK)), 0, packed, BLOCK,
    )
    arrived = scatter_blocks(packed, "row")
    returned_t = jnp.sum(arrived[:, BLOCK:].astype(f32), axis=0)

    hp = lax.Precision.HIGHEST
    combined = cotangent.astype(f32) + returned_t.T
    hidden_grad = jnp.dot(combined, second_weight.astype(f32).T, precision=hp, preferred_element_type=f32)
    pre_grad = (hidden_grad * gelu_slope(first_pre)).astype(bf16)
    first_term = jnp.dot(first_mix.T, pre_grad, preferred_element_type=f32)
    second_term = jnp.dot(hidden.astype(f32).T, combined, precision=hp, preferred_element_type=f32)
    node_scale = 1.0 / math.sqrt(node_count * n_rows_axis * n_cols_axis)
    flat = jnp.concatenate([first_term.reshape(-1), second_term.reshape(-1)]) * node_scale
    slices = flat.reshape(row_groups, -1, BLOCK)

    packed = jnp.zeros((row_groups, BLOCK + slices.shape[1], BLOCK), bf16)
    packed = forward_aggregate_into(live, rows, cols, tiles, mask, arrived, 0, slices.astype(bf16), BLOCK, packed, 0)
    arrived = scatter_blocks(packed, "col").astype(f32)
    summed_y = jnp.sum(arrived[:, :BLOCK], axis=0)
    output = (projected + row_scale * summed_y).astype(bf16)
    part = jnp.sum(arrived[:, BLOCK:], axis=0)

    total = jnp.sum(gather_blocks(part.astype(bf16), "row").astype(f32), axis=0)
    everything = gather_blocks(total.astype(bf16), "col").astype(f32).reshape(-1)
    split = first_term.size
    first_grad = everything[:split].reshape(first_term.shape)
    second_grad = everything[split:].reshape(second_term.shape)
    return (output, first_grad, second_grad)


def solution(mesh):
    return jax.shard_map(
        local,
        mesh=mesh,
        in_specs=(
            P(("row", "col"), None),
            P(),
            P(),
            P("row", "col", None),
            P("row", "col", None),
            P("row", "col"),
            P("row", "col", None, None),
            P("row", "col", None, None, None),
            P(("row", "col"), None),
        ),
        out_specs=(P(("row", "col"), None), P(), P()),
        check_vma=False,
    )
```

```python
import functools
import math

import jax
import jax.numpy as jnp
from jax import lax
from jax.experimental import pallas as pl
from jax.experimental.pallas import tpu as pltpu
from jax.sharding import PartitionSpec as P

BLOCK = 128


gelu_coef = math.sqrt(2.0 / math.pi)


def gelu_tanh(value):
    return 0.5 * value * (1.0 + jnp.tanh(gelu_coef * (value + 0.044715 * value * value * value)))


def gelu_slope(value):
    tanh_value = jnp.tanh(gelu_coef * (value + 0.044715 * value * value * value))
    return 0.5 * (1.0 + tanh_value) + 0.5 * value * (1.0 - tanh_value * tanh_value) * gelu_coef * (
        1.0 + 3.0 * 0.044715 * value * value
    )


UNROLL = 16


def _slot(k, u, n_live, slots):
    index = k * UNROLL + u
    return jnp.minimum(index, slots - 1), (index < n_live).astype(jnp.float32)


def _masked_tile(tiles_ref, mask_ref, s, keep):
    column = mask_ref[pl.ds(s, 1), :].astype(jnp.float32) * keep
    return (tiles_ref[s].astype(jnp.float32) * column).astype(jnp.bfloat16)


def _forward_kernel(row_offset, src_offset, live_ref, rows_ref, cols_ref, tiles_ref, mask_ref, src_ref, into_ref,
                    out_ref, acc_ref, stage_ref, sem):
    del into_ref
    slots = tiles_ref.shape[0]
    n_dst = acc_ref.shape[0]
    n_src = src_ref.shape[0]
    acc_ref[...] = jnp.zeros_like(acc_ref)
    n_live = jnp.clip(live_ref[0], 0, slots)

    def body(k, carry):
        for u in range(UNROLL):
            s, keep = _slot(k, u, n_live, slots)
            r = jnp.clip(rows_ref[s], 0, n_dst - 1)
            c = jnp.clip(cols_ref[s], 0, n_src - 1)
            tile = _masked_tile(tiles_ref, mask_ref, s, keep)
            source = src_ref[c, src_offset : src_offset + BLOCK, :]
            acc_ref[r] += jnp.dot(tile, source, preferred_element_type=jnp.float32)
        return carry

    lax.fori_loop(0, (n_live + UNROLL - 1) // UNROLL, body, 0)
    stage_ref[...] = acc_ref[...].astype(stage_ref.dtype)
    copy = pltpu.make_async_copy(stage_ref, out_ref.at[:, pl.ds(row_offset, BLOCK), :], sem)
    copy.start()
    copy.wait()


def _transpose_kernel(row_offset, src_offset, live_ref, rows_ref, cols_ref, tiles_ref, mask_ref, src_ref, scale_ref,
                      into_ref, out_ref, acc_ref, stage_ref, sem):
    del into_ref
    slots = tiles_ref.shape[0]
    n_dst = acc_ref.shape[0]
    n_src = src_ref.shape[0]
    acc_ref[...] = jnp.zeros_like(acc_ref)
    n_live = jnp.clip(live_ref[0], 0, slots)

    def body(k, carry):
        for u in range(UNROLL):
            s, keep = _slot(k, u, n_live, slots)
            r = jnp.clip(rows_ref[s], 0, n_src - 1)
            c = jnp.clip(cols_ref[s], 0, n_dst - 1)
            tile = _masked_tile(tiles_ref, mask_ref, s, keep)
            scale = scale_ref[pl.ds(r, 1), :]
            source = src_ref[r, src_offset : src_offset + BLOCK, :].astype(jnp.float32)
            source = (source * scale).astype(jnp.bfloat16)
            acc_ref[c] += jnp.dot(source, tile, preferred_element_type=jnp.float32)
        return carry

    lax.fori_loop(0, (n_live + UNROLL - 1) // UNROLL, body, 0)
    stage_ref[...] = acc_ref[...].astype(stage_ref.dtype)
    copy = pltpu.make_async_copy(stage_ref, out_ref.at[:, pl.ds(row_offset, BLOCK), :], sem)
    copy.start()
    copy.wait()


_SMEM = pl.BlockSpec(memory_space=pltpu.SMEM)
_VMEM = pl.BlockSpec(memory_space=pltpu.VMEM)
_ANY = pl.BlockSpec(memory_space=pl.ANY)


def _aggregate_into(kernel, operands, n_vmem, into, row_offset, src_offset, tiles, src_bytes):
    n_dst = into.shape[0]
    width = into.shape[2]
    slots = tiles.shape[0]
    flops = 2 * slots * BLOCK * BLOCK * width
    bytes_accessed = tiles.size * 2 + src_bytes + n_dst * BLOCK * width * 2
    return pl.pallas_call(
        functools.partial(kernel, row_offset, src_offset),
        out_shape=jax.ShapeDtypeStruct(into.shape, into.dtype),
        in_specs=[_SMEM, _SMEM, _SMEM] + [_VMEM] * n_vmem + [_ANY],
        out_specs=_ANY,
        scratch_shapes=[
            pltpu.VMEM((n_dst, BLOCK, width), jnp.float32),
            pltpu.VMEM((n_dst, BLOCK, width), into.dtype),
            pltpu.SemaphoreType.DMA(()),
        ],
        input_output_aliases={3 + n_vmem: 0},
        cost_estimate=pl.CostEstimate(flops=flops, bytes_accessed=bytes_accessed, transcendentals=0),
    )(*operands, into)


def forward_aggregate_into(live, rows, cols, tiles, mask, src, src_offset, into, row_offset):
    n_src = src.shape[0]
    return _aggregate_into(
        _forward_kernel, (live, rows, cols, tiles, mask, src), 3, into, row_offset, src_offset, tiles,
        n_src * BLOCK * BLOCK * 2,
    )


def transpose_aggregate_into(live, rows, cols, tiles, mask, src_t, src_offset, scale, into, row_offset):
    n_src = src_t.shape[0]
    return _aggregate_into(
        _transpose_kernel, (live, rows, cols, tiles, mask, src_t, scale), 4, into, row_offset, src_offset, tiles,
        n_src * BLOCK * BLOCK * 2,
    )


def gather_blocks(block, axis):
    n = lax.axis_size(axis)
    return lax.all_to_all(jnp.broadcast_to(block[None], (n,) + block.shape), axis, 0, 0, tiled=False)


def scatter_blocks(blocks, axis):
    return lax.all_to_all(blocks, axis, 0, 0, tiled=False)


def split_hi_lo(value):
    hi = value.astype(jnp.bfloat16)
    lo = (value - hi.astype(jnp.float32)).astype(jnp.bfloat16)
    return hi, lo


def local(
    features,
    first_weight,
    second_weight,
    tile_rows,
    tile_cols,
    tile_live,
    column_mask,
    edge_weight,
    cotangent,
):
    f32 = jnp.float32
    bf16 = jnp.bfloat16
    n_rows_axis = lax.axis_size("row")
    n_cols_axis = lax.axis_size("col")
    node_count = features.shape[0]
    row_groups = n_cols_axis * node_count // BLOCK
    col_groups = n_rows_axis * node_count // BLOCK

    live = tile_live.reshape(1)
    rows = tile_rows[0, 0]
    cols = tile_cols[0, 0]
    tiles = edge_weight[0, 0]
    mask = column_mask[0, 0]

    x_panel = gather_blocks(features, "row")
    live_weight = (jnp.arange(tiles.shape[0]) < jnp.clip(live[0], 0, tiles.shape[0])).astype(jnp.int32)
    live_mask = (mask * live_weight[:, None]).astype(bf16)
    row_sums = jnp.einsum("sij,sj->si", tiles, live_mask, preferred_element_type=f32)
    partial_deg = jnp.zeros((row_groups, BLOCK), f32).at[jnp.clip(rows, 0, row_groups - 1)].add(row_sums)
    shared = jnp.concatenate([partial_deg.astype(bf16), cotangent.T], axis=0)
    packed = jnp.concatenate(
        [jnp.zeros((row_groups, BLOCK, BLOCK), bf16), jnp.broadcast_to(shared[None], (row_groups,) + shared.shape)],
        axis=1,
    )
    packed = forward_aggregate_into(live, rows, cols, tiles, mask, x_panel, 0, packed, 0)
    arrived = scatter_blocks(packed, "col")
    summed_in = jnp.sum(arrived[:, :BLOCK].astype(f32), axis=0)
    degrees = jnp.sum(arrived[:, BLOCK : BLOCK + row_groups].astype(f32), axis=0)
    group_scale = 1.0 / jnp.sqrt(1.0 + degrees)
    me = lax.axis_index("col")
    row_scale = lax.dynamic_index_in_dim(group_scale, me, axis=0, keepdims=False)[:, None]

    first_mix = (features.astype(f32) + row_scale * summed_in).astype(bf16)
    first_pre = jnp.dot(first_mix, first_weight, preferred_element_type=f32)
    hidden = gelu_tanh(first_pre).astype(bf16)
    projected = jnp.dot(hidden, second_weight, preferred_element_type=f32)

    packed = jnp.concatenate(
        [
            jnp.broadcast_to(projected.astype(bf16)[None], (col_groups, BLOCK, BLOCK)),
            jnp.zeros((col_groups, BLOCK, BLOCK), bf16),
        ],
        axis=1,
    )
    packed = transpose_aggregate_into(
        live, rows, cols, tiles, mask, arrived, BLOCK + row_groups, group_scale, packed, BLOCK
    )
    arrived = scatter_blocks(packed, "row")
    returned_t = jnp.sum(arrived[:, BLOCK:].astype(f32), axis=0)

    combined = cotangent.astype(f32) + returned_t.T
    hidden_grad = jnp.dot(combined.astype(bf16), second_weight.T, preferred_element_type=f32)
    pre_grad = (hidden_grad * gelu_slope(first_pre)).astype(bf16)
    first_term = jnp.dot(first_mix.T, pre_grad, preferred_element_type=f32)
    second_term = jnp.dot(hidden.T, combined.astype(bf16), preferred_element_type=f32)
    node_scale = 1.0 / math.sqrt(node_count * n_rows_axis * n_cols_axis)
    flat = jnp.concatenate([first_term.reshape(-1), second_term.reshape(-1)]) * node_scale
    slices = flat.reshape(row_groups, -1, BLOCK)

    packed = jnp.concatenate([jnp.zeros((row_groups, BLOCK, BLOCK), bf16), slices.astype(bf16)], axis=1)
    packed = forward_aggregate_into(live, rows, cols, tiles, mask, arrived, 0, packed, 0)
    arrived = scatter_blocks(packed, "col").astype(f32)
    summed_y = jnp.sum(arrived[:, :BLOCK], axis=0)
    output = (projected + row_scale * summed_y).astype(bf16)
    part = jnp.sum(arrived[:, BLOCK:], axis=0)

    total = jnp.sum(gather_blocks(part.astype(bf16), "row").astype(f32), axis=0)
    everything = gather_blocks(total.astype(bf16), "col").astype(f32).reshape(-1)
    split = first_term.size
    first_grad = everything[:split].reshape(first_term.shape)
    second_grad = everything[split:].reshape(second_term.shape)
    return (output, first_grad, second_grad)


def solution(mesh):
    return jax.shard_map(
        local,
        mesh=mesh,
        in_specs=(
            P(("row", "col"), None),
            P(),
            P(),
            P("row", "col", None),
            P("row", "col", None),
            P("row", "col"),
            P("row", "col", None, None),
            P("row", "col", None, None, None),
            P(("row", "col"), None),
        ),
        out_specs=(P(("row", "col"), None), P(), P()),
        check_vma=False,
    )
```

```python
import functools
import math

import jax
import jax.numpy as jnp
from jax import lax
from jax.experimental import pallas as pl
from jax.experimental.pallas import tpu as pltpu
from jax.sharding import PartitionSpec as P

BLOCK = 128


gelu_coef = math.sqrt(2.0 / math.pi)


def gelu_tanh(value):
    return 0.5 * value * (1.0 + jnp.tanh(gelu_coef * (value + 0.044715 * value * value * value)))


def gelu_slope(value):
    tanh_value = jnp.tanh(gelu_coef * (value + 0.044715 * value * value * value))
    return 0.5 * (1.0 + tanh_value) + 0.5 * value * (1.0 - tanh_value * tanh_value) * gelu_coef * (
        1.0 + 3.0 * 0.044715 * value * value
    )


UNROLL = 20


def _slot(k, u, n_live, slots):
    index = k * UNROLL + u
    return jnp.minimum(index, slots - 1), (index < n_live).astype(jnp.float32)


def _masked_tile(tiles_ref, mask_ref, s, keep):
    column = mask_ref[pl.ds(s, 1), :].astype(jnp.float32) * keep
    return (tiles_ref[s].astype(jnp.float32) * column).astype(jnp.bfloat16)


def _forward_kernel(row_offset, src_offset, live_ref, rows_ref, cols_ref, tiles_ref, mask_ref, src_ref, into_ref,
                    out_ref, acc_ref, stage_ref, sem):
    del into_ref
    slots = tiles_ref.shape[0]
    n_dst = acc_ref.shape[0]
    n_src = src_ref.shape[0]
    acc_ref[...] = jnp.zeros_like(acc_ref)
    n_live = jnp.clip(live_ref[0], 0, slots)

    def body(k, carry):
        for u in range(UNROLL):
            s, keep = _slot(k, u, n_live, slots)
            r = jnp.clip(rows_ref[s], 0, n_dst - 1)
            c = jnp.clip(cols_ref[s], 0, n_src - 1)
            tile = _masked_tile(tiles_ref, mask_ref, s, keep)
            source = src_ref[c, src_offset : src_offset + BLOCK, :]
            acc_ref[r] += jnp.dot(tile, source, preferred_element_type=jnp.float32)
        return carry

    lax.fori_loop(0, (n_live + UNROLL - 1) // UNROLL, body, 0)
    stage_ref[...] = acc_ref[...].astype(stage_ref.dtype)
    copy = pltpu.make_async_copy(stage_ref, out_ref.at[:, pl.ds(row_offset, BLOCK), :], sem)
    copy.start()
    copy.wait()


def _transpose_kernel(row_offset, src_offset, live_ref, rows_ref, cols_ref, tiles_ref, mask_ref, src_ref, scale_ref,
                      into_ref, out_ref, acc_ref, stage_ref, sem):
    del into_ref
    slots = tiles_ref.shape[0]
    n_dst = acc_ref.shape[0]
    n_src = src_ref.shape[0]
    acc_ref[...] = jnp.zeros_like(acc_ref)
    n_live = jnp.clip(live_ref[0], 0, slots)

    def body(k, carry):
        for u in range(UNROLL):
            s, keep = _slot(k, u, n_live, slots)
            r = jnp.clip(rows_ref[s], 0, n_src - 1)
            c = jnp.clip(cols_ref[s], 0, n_dst - 1)
            tile = _masked_tile(tiles_ref, mask_ref, s, keep)
            scale = scale_ref[pl.ds(r, 1), :]
            source = src_ref[r, src_offset : src_offset + BLOCK, :].astype(jnp.float32)
            source = (source * scale).astype(jnp.bfloat16)
            acc_ref[c] += jnp.dot(source, tile, preferred_element_type=jnp.float32)
        return carry

    lax.fori_loop(0, (n_live + UNROLL - 1) // UNROLL, body, 0)
    stage_ref[...] = acc_ref[...].astype(stage_ref.dtype)
    copy = pltpu.make_async_copy(stage_ref, out_ref.at[:, pl.ds(row_offset, BLOCK), :], sem)
    copy.start()
    copy.wait()


_SMEM = pl.BlockSpec(memory_space=pltpu.SMEM)
_VMEM = pl.BlockSpec(memory_space=pltpu.VMEM)
_ANY = pl.BlockSpec(memory_space=pl.ANY)


def _aggregate_into(kernel, operands, n_vmem, into, row_offset, src_offset, tiles, src_bytes):
    n_dst = into.shape[0]
    width = into.shape[2]
    slots = tiles.shape[0]
    flops = 2 * slots * BLOCK * BLOCK * width
    bytes_accessed = tiles.size * 2 + src_bytes + n_dst * BLOCK * width * 2
    return pl.pallas_call(
        functools.partial(kernel, row_offset, src_offset),
        out_shape=jax.ShapeDtypeStruct(into.shape, into.dtype),
        in_specs=[_SMEM, _SMEM, _SMEM] + [_VMEM] * n_vmem + [_ANY],
        out_specs=_ANY,
        scratch_shapes=[
            pltpu.VMEM((n_dst, BLOCK, width), jnp.float32),
            pltpu.VMEM((n_dst, BLOCK, width), into.dtype),
            pltpu.SemaphoreType.DMA(()),
        ],
        input_output_aliases={3 + n_vmem: 0},
        cost_estimate=pl.CostEstimate(flops=flops, bytes_accessed=bytes_accessed, transcendentals=0),
    )(*operands, into)


def forward_aggregate_into(live, rows, cols, tiles, mask, src, src_offset, into, row_offset):
    n_src = src.shape[0]
    return _aggregate_into(
        _forward_kernel, (live, rows, cols, tiles, mask, src), 3, into, row_offset, src_offset, tiles,
        n_src * BLOCK * BLOCK * 2,
    )


def transpose_aggregate_into(live, rows, cols, tiles, mask, src_t, src_offset, scale, into, row_offset):
    n_src = src_t.shape[0]
    return _aggregate_into(
        _transpose_kernel, (live, rows, cols, tiles, mask, src_t, scale), 4, into, row_offset, src_offset, tiles,
        n_src * BLOCK * BLOCK * 2,
    )


def gather_blocks(block, axis):
    n = lax.axis_size(axis)
    return lax.all_to_all(jnp.broadcast_to(block[None], (n,) + block.shape), axis, 0, 0, tiled=False)


def scatter_blocks(blocks, axis):
    return lax.all_to_all(blocks, axis, 0, 0, tiled=False)


def split_hi_lo(value):
    hi = value.astype(jnp.bfloat16)
    lo = (value - hi.astype(jnp.float32)).astype(jnp.bfloat16)
    return hi, lo


def local(
    features,
    first_weight,
    second_weight,
    tile_rows,
    tile_cols,
    tile_live,
    column_mask,
    edge_weight,
    cotangent,
):
    f32 = jnp.float32
    bf16 = jnp.bfloat16
    n_rows_axis = lax.axis_size("row")
    n_cols_axis = lax.axis_size("col")
    node_count = features.shape[0]
    row_groups = n_cols_axis * node_count // BLOCK
    col_groups = n_rows_axis * node_count // BLOCK

    live = tile_live.reshape(1)
    rows = tile_rows[0, 0]
    cols = tile_cols[0, 0]
    tiles = edge_weight[0, 0]
    mask = column_mask[0, 0]

    x_panel = gather_blocks(features, "row")
    live_weight = (jnp.arange(tiles.shape[0]) < jnp.clip(live[0], 0, tiles.shape[0])).astype(jnp.int32)
    live_mask = (mask * live_weight[:, None]).astype(bf16)
    row_sums = jnp.einsum("sij,sj->si", tiles, live_mask, preferred_element_type=f32)
    partial_deg = jnp.zeros((row_groups, BLOCK), f32).at[jnp.clip(rows, 0, row_groups - 1)].add(row_sums)
    shared = jnp.concatenate([partial_deg.astype(bf16), cotangent.T], axis=0)
    packed = jnp.concatenate(
        [jnp.zeros((row_groups, BLOCK, BLOCK), bf16), jnp.broadcast_to(shared[None], (row_groups,) + shared.shape)],
        axis=1,
    )
    packed = forward_aggregate_into(live, rows, cols, tiles, mask, x_panel, 0, packed, 0)
    arrived = scatter_blocks(packed, "col")
    summed_in = jnp.sum(arrived[:, :BLOCK].astype(f32), axis=0)
    degrees = jnp.sum(arrived[:, BLOCK : BLOCK + row_groups].astype(f32), axis=0)
    group_scale = 1.0 / jnp.sqrt(1.0 + degrees)
    me = lax.axis_index("col")
    row_scale = lax.dynamic_index_in_dim(group_scale, me, axis=0, keepdims=False)[:, None]

    first_mix = (features.astype(f32) + row_scale * summed_in).astype(bf16)
    first_pre = jnp.dot(first_mix, first_weight, preferred_element_type=f32)
    hidden = gelu_tanh(first_pre).astype(bf16)
    projected = jnp.dot(hidden, second_weight, preferred_element_type=f32)

    packed = jnp.concatenate(
        [
            jnp.broadcast_to(projected.astype(bf16)[None], (col_groups, BLOCK, BLOCK)),
            jnp.zeros((col_groups, BLOCK, BLOCK), bf16),
        ],
        axis=1,
    )
    packed = transpose_aggregate_into(
        live, rows, cols, tiles, mask, arrived, BLOCK + row_groups, group_scale, packed, BLOCK
    )
    arrived = scatter_blocks(packed, "row")
    returned_t = jnp.sum(arrived[:, BLOCK:].astype(f32), axis=0)

    combined = cotangent.astype(f32) + returned_t.T
    hidden_grad = jnp.dot(combined.astype(bf16), second_weight.T, preferred_element_type=f32)
    pre_grad = (hidden_grad * gelu_slope(first_pre)).astype(bf16)
    first_term = jnp.dot(first_mix.T, pre_grad, preferred_element_type=f32)
    second_term = jnp.dot(hidden.T, combined.astype(bf16), preferred_element_type=f32)
    node_scale = 1.0 / math.sqrt(node_count * n_rows_axis * n_cols_axis)
    flat = jnp.concatenate([first_term.reshape(-1), second_term.reshape(-1)]) * node_scale
    slices = flat.reshape(row_groups, -1, BLOCK)

    packed = jnp.concatenate([jnp.zeros((row_groups, BLOCK, BLOCK), bf16), slices.astype(bf16)], axis=1)
    packed = forward_aggregate_into(live, rows, cols, tiles, mask, arrived, 0, packed, 0)
    arrived = scatter_blocks(packed, "col").astype(f32)
    summed_y = jnp.sum(arrived[:, :BLOCK], axis=0)
    output = (projected + row_scale * summed_y).astype(bf16)
    part = jnp.sum(arrived[:, BLOCK:], axis=0)

    total = jnp.sum(gather_blocks(part.astype(bf16), "row").astype(f32), axis=0)
    everything = gather_blocks(total.astype(bf16), "col").astype(f32).reshape(-1)
    split = first_term.size
    first_grad = everything[:split].reshape(first_term.shape)
    second_grad = everything[split:].reshape(second_term.shape)
    return (output, first_grad, second_grad)


def solution(mesh):
    return jax.shard_map(
        local,
        mesh=mesh,
        in_specs=(
            P(("row", "col"), None),
            P(),
            P(),
            P("row", "col", None),
            P("row", "col", None),
            P("row", "col"),
            P("row", "col", None, None),
            P("row", "col", None, None, None),
            P(("row", "col"), None),
        ),
        out_specs=(P(("row", "col"), None), P(), P()),
        check_vma=False,
    )
```
